32 devices in a mesh: layer: 4 (over y, x), tok: 8 (over z, core).
Axes of the slice: x: 2, y: 2, z: 4, core: 2. Of those that a mesh axis runs over, the one named last changes fastest.
Arguments:
- residual: bfloat16 [4, 1024, 3584], P('layer', 'tok'), may hold values from -6 to 6
- targets: bfloat16 [4, 1024, 3584], P('layer', 'tok'), may hold values from -6 to 6
- block_ids: int32 [4, 1024, 2], P(None, 'tok'), may hold values from 0 to 127, all different within a row; in each aligned block of 128 rows (0 to 127, 128 to 255, ..., all dimensions but the last counted through in order) at most 4 rows name the same one
- encoder_weight: bfloat16 [4, 3584, 16384], P('layer', None, 'tok'), may hold values from -0.09375 to 0.09375
- encoder_bias: float32 [4, 16384], P('layer', 'tok'), may hold values from -3 to 3
- decoder_weight: bfloat16 [4, 4, 16384, 3584], P('layer', None, 'tok'), may hold values from -0.25 to 0.25
- decoder_bias: float32 [4, 3584], P('layer'), may hold values from -3 to 3
Outputs:
- reconstruction: bfloat16 [4, 1024, 3584], P('layer', 'tok')
- error: float32 [4, 1024], P('layer', 'tok')
The draws below stay inside these ranges and needn't reach their ends.
Inputs may be any that keep to these rules, and one draw needn't show every extreme that they name: `block_ids`: A token's 2 blocks in a layer are distinct. In each layer, the 128 rows of one device (aligned blocks of tokens) name no block more than 4 times, and some block exactly 4 times.
All inputs are finite; a program needn't handle non-finite values.
Results may differ from the reference program's by a relative error of at most 0.0053.
Values may be sent and summed in bfloat16 or wider, within the bound.
No kernel may reach another device: no remote copies, remote signals or barrier semaphores. Data moves between devices by JAX's collectives and lax.ppermute only.
A program may use at most 192 MiB of HBM per device.

```python
import math
import jax
import jax.numpy as jnp
import numpy as np
from jax import lax

D = 3584
F = 16384
BLOCK = 128
K = 2
TOK_DEV = 128
CAP = 4
LAYERS = 4
TOKENS = 1024
N_TOK = 8


def levels(rng, dims, split, low, high):
    def one(dim, blocks):
        heights = jax.random.uniform(jax.random.fold_in(jax.random.fold_in(rng, 6), dim), (blocks,), jnp.float32, low / len(split), high / len(split))
        return jnp.repeat(jnp.exp(heights), dims[dim] // blocks).reshape((-1,) + (1,) * (len(dims) - dim - 1))

    level = one(*split[0])
    for cut in split[1:]:
        level = level * one(*cut)
    return level


def assign_block(rng, own, number, rows, number_of, top, reach, skew):
    order = jax.random.permutation(rng, number_of)
    packed, ordinary = shares(number_of, rows * top, reach, skew, True), shares(number_of, rows * top, reach, skew, False)
    places = jnp.arange(number_of)

    def named(lengths, offset_by):
        used = int((lengths > 0).sum())
        fixed = max(1, used // 4)
        passed = fixed + (places - fixed + offset_by * (used - fixed)) % max(1, number_of - fixed)
        return jnp.zeros((number_of,), jnp.int32).at[order[jnp.where(places < fixed, places, passed)]].set(jnp.asarray(lengths, jnp.int32))

    lengths = jnp.where(number % 4 == 0, named(packed, number // 4), named(ordinary, number - number // 4 - 1))
    mixed = jax.random.permutation(jax.random.fold_in(own, 3), number_of)
    giver, receiver = mixed[0:number_of // 2 * 2:2], mixed[1:number_of // 2 * 2:2]
    margin = jnp.minimum(lengths[giver] - 1, reach - lengths[receiver]) // 2
    margin = jnp.where((giver == order[0]) | (receiver == order[0]) | (lengths[receiver] == 0), 0, jnp.maximum(margin, 0))
    passed = jax.random.randint(jax.random.fold_in(own, 4), (number_of // 2,), 0, 1 << 20) % (margin + 1)
    lengths = lengths.at[giver].add(-passed).at[receiver].add(passed)
    members = jnp.searchsorted(jnp.cumsum(lengths), jnp.arange(rows * top), side="right").astype(jnp.int32)
    grid = members.reshape(top, rows).T
    grid = grid[jax.random.permutation(jax.random.fold_in(own, 1), rows)]
    offset_by = jax.random.randint(jax.random.fold_in(own, 2), (rows, 1), 0, top)
    return jnp.take_along_axis(grid, (jnp.arange(top)[None, :] + offset_by) % top, axis=1)


def shares(count, total, limit, lean, full):
    portions = [(1 << 20) // math.isqrt(rank ** lean) + 1 for rank in range(1, count + 1)]
    largest = limit if full else min(limit, max(-(-total // count), total * portions[0] // sum(portions)))
    least = 1 if total - largest >= count - 1 else 0
    given, spare = [largest] + [least] * (count - 1), total - largest - least * (count - 1)
    while spare > 0:
        movable = [i for i in range(1, count) if given[i] < largest] or [i for i in range(1, count) if given[i] < limit]
        pool, budget = sum([portions[i] for i in movable]), spare
        for i in movable:
            more = min(limit - given[i], max(1, budget * portions[i] // pool), spare)
            given[i] = given[i] + more
            spare = spare - more
    return np.array(given)


def bell_draw(key, dims, deviation, reach, pieces=(), kind=jnp.bfloat16):
    array = jax.random.normal(key, dims, jnp.float32) * deviation
    if len(pieces) > 0:
        array = levels(key, dims, pieces, -0.22, 0.18) * array
    return jnp.clip(array, min=-reach, max=reach).astype(kind)


def setup_inputs(seed: int = 0) -> dict:
    streams_of = jax.random.split(jax.random.key(seed), 8)
    residual = bell_draw(streams_of[0], (LAYERS, TOKENS, D), 1.0, 6.0, ((0, 4), (1, 8)))
    targets = bell_draw(streams_of[1], (LAYERS, TOKENS, D), 1.0, 6.0, ((0, 4), (1, 8)))
    block_ids_keys = jax.random.split(jax.random.fold_in(streams_of[2], 1), LAYERS * TOKENS // TOK_DEV)
    block_ids_turns = jax.random.permutation(jax.random.fold_in(streams_of[2], 3), LAYERS * TOKENS // TOK_DEV)
    block_ids = jax.vmap(lambda own, number: assign_block(jax.random.fold_in(streams_of[2], 2), own, number, TOK_DEV, F // BLOCK, K, CAP, 2))(block_ids_keys, block_ids_turns).reshape((LAYERS, TOKENS, K))
    encoder_weight = bell_draw(streams_of[3], (LAYERS, D, F), D ** -0.5, 0.09375, ((0, 4), (2, 8)))
    encoder_bias = bell_draw(streams_of[4], (LAYERS, F), 0.5, 3.0, ((0, 4), (1, 8)), jnp.float32)
    decoder_weight = bell_draw(streams_of[5], (LAYERS, LAYERS, F, D), (2 * K * BLOCK) ** -0.5, 0.25, ((0, 4), (2, 8)))
    decoder_bias = bell_draw(streams_of[6], (LAYERS, D), 0.5, 3.0, ((0, 4),), jnp.float32)
    return {"residual": residual, "targets": targets, "block_ids": block_ids, "encoder_weight": encoder_weight, "encoder_bias": encoder_bias, "decoder_weight": decoder_weight, "decoder_bias": decoder_bias}


def slot_table(flat_ids, blocks, room):
    onehot = (flat_ids[:, None] == jnp.arange(blocks, dtype=jnp.int32)[None, :]).astype(jnp.int32)
    rank_in = jnp.sum((jnp.cumsum(onehot, axis=0) - onehot) * onehot, axis=1).astype(jnp.int32)
    token_of = (jnp.arange(TOKENS * K, dtype=jnp.int32) // K).astype(jnp.int32)
    table = jnp.full((blocks, room), TOKENS, jnp.int32)
    return table.at[flat_ids, rank_in].set(token_of)


def reference(residual, targets, block_ids, encoder_weight, encoder_bias, decoder_weight, decoder_bias):
    blocks = F // BLOCK
    room = N_TOK * CAP
    tables = []
    all_codes = []
    for layer in range(LAYERS):
        table = slot_table(block_ids[layer].reshape(-1).astype(jnp.int32), blocks, room)
        padded = jnp.concatenate([residual[layer], jnp.zeros((1, D), residual.dtype)], axis=0)
        enc_blocks = encoder_weight[layer].reshape(D, blocks, BLOCK).transpose(1, 0, 2)
        bias_blocks = encoder_bias[layer].reshape(blocks, BLOCK)

        def encode(items, padded=padded):
            rows, weight_block, bias_block = items
            pre = jnp.dot(padded[rows], weight_block, preferred_element_type=jnp.float32) + bias_block
            return jnp.maximum(pre, 0.0).astype(jnp.bfloat16)

        all_codes.append(lax.map(encode, (table, enc_blocks, bias_blocks)))
        tables.append(table)
    recon_list = []
    error_list = []
    for target in range(LAYERS):
        total = jnp.zeros((TOKENS + 1, D), jnp.float32)
        for source in range(target + 1):
            dec_blocks = decoder_weight[target, source].reshape(blocks, BLOCK, D)

            def add_block(running, items):
                rows, code_block, weight_block = items
                term = jnp.dot(code_block, weight_block, preferred_element_type=jnp.float32).astype(jnp.bfloat16)
                term = lax.optimization_barrier(term).astype(jnp.float32)
                return running.at[rows].add(term), None

            total, _ = lax.scan(add_block, total, (tables[source], all_codes[source], dec_blocks))
        recon32 = decoder_bias[target][None, :] + total[:TOKENS]
        recon_list.append(recon32.astype(jnp.bfloat16))
        diff = recon32 - targets[target].astype(jnp.float32)
        error_list.append(jnp.mean(diff * diff, axis=1))
    return jnp.stack(recon_list), jnp.stack(error_list)
```

```python
import jax
import jax.numpy as jnp
from jax import lax
from jax.sharding import PartitionSpec as P

BLOCK = 128


def owner_tables(ids_all, owner, per_owner, capacity, tokens):
    layers, _, topk = ids_all.shape
    local = ids_all.reshape(layers, tokens * topk) - owner * per_owner
    owned = (local >= 0) & (local < per_owner)
    onehot = (local[..., None] == jnp.arange(per_owner, dtype=jnp.int32)).astype(jnp.int32)
    rank = jnp.sum((jnp.cumsum(onehot, axis=1) - onehot) * onehot, axis=2)
    slot_count = per_owner * capacity
    slot = jnp.where(owned, local * capacity + rank, slot_count)
    token_of = jnp.arange(tokens * topk, dtype=jnp.int32) // topk
    empty = jnp.full((slot_count,), tokens, jnp.int32)
    return jax.vmap(lambda s: empty.at[s].set(token_of, mode="drop"))(slot)


def body(residual, targets, block_ids, encoder_weight, encoder_bias, decoder_weight, decoder_bias):
    layer_index = lax.axis_index("layer")
    tok_index = lax.axis_index("tok")
    layers = lax.axis_size("layer")
    tok_count = lax.axis_size("tok")
    tok_rows = residual.shape[1]
    width = residual.shape[2]
    topk = block_ids.shape[2]
    per_owner = encoder_weight.shape[2] // BLOCK
    blocks = per_owner * tok_count
    capacity = max(2, 2 * tok_rows * topk // blocks) * tok_count
    slot_count = per_owner * capacity
    tokens = tok_rows * tok_count

    ids_all = lax.all_gather(block_ids, "tok", axis=1, tiled=True)
    table = owner_tables(ids_all, tok_index, per_owner, capacity, tokens)

    res_all = lax.all_gather(residual[0], "tok", axis=0, tiled=True)
    own_table = lax.dynamic_index_in_dim(table, layer_index, 0, keepdims=False)
    rows = jnp.take(res_all, jnp.minimum(own_table, tokens - 1), axis=0)
    enc_blocks = encoder_weight[0].reshape(width, per_owner, BLOCK)
    pre = jnp.einsum(
        "bcd,dbe->bce",
        rows.reshape(per_owner, capacity, width),
        enc_blocks,
        preferred_element_type=jnp.float32,
    )
    pre = pre + encoder_bias[0].reshape(per_owner, 1, BLOCK)
    codes = jnp.maximum(pre, 0.0).astype(jnp.bfloat16)
    all_codes = lax.all_gather(codes, "layer", axis=0, tiled=False)

    terms = jnp.einsum(
        "sbce,sbed->sbcd",
        all_codes,
        decoder_weight[0].reshape(layers, per_owner, BLOCK, width),
        preferred_element_type=jnp.float32,
    ).astype(jnp.bfloat16)
    valid = jnp.arange(layers, dtype=jnp.int32) <= layer_index
    scatter = (table[:, :, None] == jnp.arange(tokens, dtype=jnp.int32)[None, None, :]) & valid[:, None, None]
    partial = jnp.einsum(
        "sct,scd->td",
        scatter.astype(jnp.bfloat16),
        terms.reshape(layers, slot_count, width),
        preferred_element_type=jnp.float32,
    )
    summed = lax.psum_scatter(partial.astype(jnp.bfloat16), "tok", scatter_dimension=0, tiled=True)
    recon32 = decoder_bias[0][None, :] + summed.astype(jnp.float32)
    difference = recon32 - targets[0].astype(jnp.float32)
    error = jnp.mean(difference * difference, axis=1)
    return (recon32.astype(jnp.bfloat16)[None], error[None])


def solution(mesh):
    in_specs = (
        P("layer", "tok", None),
        P("layer", "tok", None),
        P(None, "tok", None),
        P("layer", None, "tok"),
        P("layer", "tok"),
        P("layer", None, "tok", None),
        P("layer", None),
    )
    out_specs = (P("layer", "tok", None), P("layer", "tok"))
    return jax.shard_map(body, mesh=mesh, in_specs=in_specs, out_specs=out_specs, check_vma=False)
```

```python
import math

import jax
import jax.numpy as jnp
from jax import lax
from jax.experimental import pallas as pl
from jax.sharding import PartitionSpec as P

BLOCK = 128


def encode_kernel(rows_ref, w_ref, b_ref, o_ref):
    group = rows_ref.shape[0]
    for i in range(group):
        cols = slice(i * BLOCK, (i + 1) * BLOCK)
        acc = jnp.dot(rows_ref[i], w_ref[:, cols], preferred_element_type=jnp.float32)
        acc = acc + b_ref[:, cols]
        o_ref[i] = jnp.maximum(acc, 0.0).astype(o_ref.dtype)


def encode(rows, weight, bias):
    per_owner, capacity, width = rows.shape
    group = math.gcd(per_owner, 4)
    return pl.pallas_call(
        encode_kernel,
        grid=(per_owner // group,),
        in_specs=[
            pl.BlockSpec((group, capacity, width), lambda g: (g, 0, 0)),
            pl.BlockSpec((width, group * BLOCK), lambda g: (0, g)),
            pl.BlockSpec((1, group * BLOCK), lambda g: (0, g)),
        ],
        out_specs=pl.BlockSpec((group, capacity, BLOCK), lambda g: (g, 0, 0)),
        out_shape=jax.ShapeDtypeStruct((per_owner, capacity, BLOCK), jnp.bfloat16),
    )(rows, weight, bias)


def pair_slots(ids, per_owner, cap):
    layers = ids.shape[0]
    flat = ids.reshape(layers, -1)
    n = flat.shape[1]
    earlier = jnp.arange(n, dtype=jnp.int32)[None, :] < jnp.arange(n, dtype=jnp.int32)[:, None]
    same = (flat[:, :, None] == flat[:, None, :]) & earlier[None]
    rank = jnp.sum(same.astype(jnp.int32), axis=2)
    return (flat * cap + rank).reshape(ids.shape)


def body(residual, targets, block_ids, encoder_weight, encoder_bias, decoder_weight, decoder_bias):
    layer_index = lax.axis_index("layer")
    tok_index = lax.axis_index("tok")
    layers = lax.axis_size("layer")
    tok_count = lax.axis_size("tok")
    tok_rows = residual.shape[1]
    width = residual.shape[2]
    topk = block_ids.shape[2]
    per_owner = encoder_weight.shape[2] // BLOCK
    blocks = per_owner * tok_count
    cap = max(2, 2 * tok_rows * topk // blocks)
    per_src = per_owner * cap
    tokens = tok_rows * tok_count

    codes_own = pair_slots(block_ids, per_owner, cap)
    codes_all = lax.all_gather(codes_own, "tok", axis=1, tiled=True)
    local = codes_all.reshape(layers, tok_count, tok_rows, topk) - tok_index * per_src
    hit = local[..., None] == jnp.arange(per_src, dtype=jnp.int32)
    pick = jnp.any(hit, axis=3)

    res_all = lax.all_gather(residual[0], "tok", axis=0, tiled=True).reshape(tok_count, tok_rows, width)
    own_pick = lax.dynamic_index_in_dim(pick, layer_index, 0, keepdims=False).astype(jnp.bfloat16)
    rows = jnp.einsum("stx,std->sxd", own_pick, res_all, preferred_element_type=jnp.float32).astype(jnp.bfloat16)
    rows = rows.reshape(tok_count, per_owner, cap, width).transpose(1, 0, 2, 3).reshape(per_owner, tok_count * cap, width)
    codes = encode(rows, encoder_weight[0], encoder_bias[0].reshape(1, -1))
    gathered = lax.all_gather(codes, "layer", axis=0, tiled=False)

    terms = jnp.einsum(
        "lbxe,lbed->lbxd",
        gathered,
        decoder_weight[0].reshape(layers, per_owner, BLOCK, width),
        preferred_element_type=jnp.float32,
    ).astype(jnp.bfloat16)
    terms = terms.reshape(layers, per_owner, tok_count, cap, width)
    valid = jnp.arange(layers, dtype=jnp.int32) <= layer_index
    combine = (pick & valid[:, None, None, None]).astype(jnp.bfloat16).reshape(layers, tok_count, tok_rows, per_owner, cap)
    partial = jnp.einsum("lstbr,lbsrd->std", combine, terms, preferred_element_type=jnp.float32)
    partial = partial.reshape(tokens, width).astype(jnp.bfloat16)
    summed = lax.psum_scatter(partial, "tok", scatter_dimension=0, tiled=True)
    recon32 = decoder_bias[0][None, :] + summed.astype(jnp.float32)
    difference = recon32 - targets[0].astype(jnp.float32)
    error = jnp.mean(difference * difference, axis=1)
    return (recon32.astype(jnp.bfloat16)[None], error[None])


def solution(mesh):
    in_specs = (
        P("layer", "tok", None),
        P("layer", "tok", None),
        P(None, "tok", None),
        P("layer", None, "tok"),
        P("layer", "tok"),
        P("layer", None, "tok", None),
        P("layer", None),
    )
    out_specs = (P("layer", "tok", None), P("layer", "tok"))
    return jax.shard_map(body, mesh=mesh, in_specs=in_specs, out_specs=out_specs, check_vma=False)
```

```python
import math

import jax
import jax.numpy as jnp
from jax import lax
from jax.experimental import pallas as pl
from jax.sharding import PartitionSpec as P

BLOCK = 128


def encode_kernel(rows_ref, w_ref, b_ref, o_ref):
    group = rows_ref.shape[0]
    for i in range(group):
        cols = slice(i * BLOCK, (i + 1) * BLOCK)
        acc = jnp.dot(rows_ref[i], w_ref[:, cols], preferred_element_type=jnp.float32)
        acc = acc + b_ref[:, cols]
        o_ref[i] = jnp.maximum(acc, 0.0).astype(o_ref.dtype)


def encode(rows, weight, bias):
    per_owner, capacity, width = rows.shape
    group = math.gcd(per_owner, 4)
    return pl.pallas_call(
        encode_kernel,
        grid=(per_owner // group,),
        in_specs=[
            pl.BlockSpec((group, capacity, width), lambda g: (g, 0, 0)),
            pl.BlockSpec((width, group * BLOCK), lambda g: (0, g)),
            pl.BlockSpec((1, group * BLOCK), lambda g: (0, g)),
        ],
        out_specs=pl.BlockSpec((group, capacity, BLOCK), lambda g: (g, 0, 0)),
        out_shape=jax.ShapeDtypeStruct((per_owner, capacity, BLOCK), jnp.bfloat16),
    )(rows, weight, bias)


def pair_slots(ids, per_owner, cap):
    layers = ids.shape[0]
    flat = ids.reshape(layers, -1)
    n = flat.shape[1]
    earlier = jnp.arange(n, dtype=jnp.int32)[None, :] < jnp.arange(n, dtype=jnp.int32)[:, None]
    same = (flat[:, :, None] == flat[:, None, :]) & earlier[None]
    rank = jnp.sum(same.astype(jnp.int32), axis=2)
    return (flat * cap + rank).reshape(ids.shape)


def body(residual, targets, block_ids, encoder_weight, encoder_bias, decoder_weight, decoder_bias):
    layer_index = lax.axis_index("layer")
    tok_index = lax.axis_index("tok")
    layers = lax.axis_size("layer")
    tok_count = lax.axis_size("tok")
    tok_rows = residual.shape[1]
    width = residual.shape[2]
    topk = block_ids.shape[2]
    per_owner = encoder_weight.shape[2] // BLOCK
    blocks = per_owner * tok_count
    cap = max(2, 2 * tok_rows * topk // blocks)
    per_src = per_owner * cap
    tokens = tok_rows * tok_count
    slot_count = per_owner * tok_count * cap

    codes_own = pair_slots(block_ids, per_owner, cap)
    codes_all = lax.all_gather(codes_own, "tok", axis=1, tiled=True)
    local = codes_all.reshape(layers, tok_count, tok_rows, topk) - tok_index * per_src
    src_of = jnp.arange(tok_count, dtype=jnp.int32)[:, None]
    slot_of = jnp.where(
        (local >= 0) & (local < per_src),
        (local // cap) * (tok_count * cap) + src_of[None, :, :, None] * cap + local % cap,
        slot_count,
    ).reshape(layers, tokens, topk)
    onehot = jnp.any(slot_of[..., None] == jnp.arange(slot_count, dtype=jnp.int32), axis=2)

    res_all = lax.all_gather(residual[0], "tok", axis=0, tiled=True)
    own_onehot = lax.dynamic_index_in_dim(onehot, layer_index, 0, keepdims=False).astype(jnp.bfloat16)
    rows = jnp.einsum("tx,td->xd", own_onehot, res_all, preferred_element_type=jnp.float32).astype(jnp.bfloat16)
    codes = encode(rows.reshape(per_owner, tok_count * cap, width), encoder_weight[0], encoder_bias[0].reshape(1, -1))
    gathered = lax.all_gather(codes, "layer", axis=0, tiled=False)

    valid = jnp.arange(layers, dtype=jnp.int32) <= layer_index
    combine = (onehot & valid[:, None, None]).astype(jnp.bfloat16)
    weights = decoder_weight[0].reshape(layers, per_owner, BLOCK, width)
    chunks = 4 if width % (4 * BLOCK) == 0 else 1
    step = width // chunks
    pieces = []
    for c in range(chunks):
        terms = jnp.einsum(
            "lbxe,lbed->lbxd",
            gathered,
            weights[..., c * step:(c + 1) * step],
            preferred_element_type=jnp.float32,
        ).astype(jnp.bfloat16)
        partial = jnp.einsum(
            "ltx,lxd->td",
            combine,
            terms.reshape(layers, slot_count, step),
            preferred_element_type=jnp.float32,
        ).astype(jnp.bfloat16)
        pieces.append(lax.psum_scatter(partial, "tok", scatter_dimension=0, tiled=True))
    summed = jnp.concatenate(pieces, axis=1)
    recon32 = decoder_bias[0][None, :] + summed.astype(jnp.float32)
    difference = recon32 - targets[0].astype(jnp.float32)
    error = jnp.mean(difference * difference, axis=1)
    return (recon32.astype(jnp.bfloat16)[None], error[None])


def solution(mesh):
    in_specs = (
        P("layer", "tok", None),
        P("layer", "tok", None),
        P(None, "tok", None),
        P("layer", None, "tok"),
        P("layer", "tok"),
        P("layer", None, "tok", None),
        P("layer", None),
    )
    out_specs = (P("layer", "tok", None), P("layer", "tok"))
    return jax.shard_map(body, mesh=mesh, in_specs=in_specs, out_specs=out_specs, check_vma=False)
```

```python
import math

import jax
import jax.numpy as jnp
from jax import lax
from jax.experimental import pallas as pl
from jax.experimental.pallas import tpu as pltpu
from jax.sharding import PartitionSpec as P

BLOCK = 128


def encode_kernel(rows_ref, w_ref, b_ref, o_ref):
    group = rows_ref.shape[0]
    for i in range(group):
        cols = slice(i * BLOCK, (i + 1) * BLOCK)
        acc = jnp.dot(rows_ref[i], w_ref[:, cols], preferred_element_type=jnp.float32)
        acc = acc + b_ref[:, cols]
        o_ref[i] = jnp.maximum(acc, 0.0).astype(o_ref.dtype)


def encode(rows, weight, bias):
    per_owner, capacity, width = rows.shape
    group = math.gcd(per_owner, 4)
    return pl.pallas_call(
        encode_kernel,
        grid=(per_owner // group,),
        in_specs=[
            pl.BlockSpec((group, capacity, width), lambda g: (g, 0, 0)),
            pl.BlockSpec((width, group * BLOCK), lambda g: (0, g)),
            pl.BlockSpec((1, group * BLOCK), lambda g: (0, g)),
        ],
        out_specs=pl.BlockSpec((group, capacity, BLOCK), lambda g: (g, 0, 0)),
        out_shape=jax.ShapeDtypeStruct((per_owner, capacity, BLOCK), jnp.bfloat16),
    )(rows, weight, bias)


def decode_kernel(codes_ref, w_ref, c_ref, o_ref, t_ref, acc_ref):
    l = pl.program_id(1)
    b = pl.program_id(2)
    rows = codes_ref.shape[2]
    term = jnp.dot(codes_ref[0, 0], w_ref[0], preferred_element_type=jnp.float32)
    t_ref[pl.ds(pl.multiple_of(b * rows, rows), rows), :] = term.astype(t_ref.dtype)

    @pl.when(b == pl.num_programs(2) - 1)
    def _():
        width = t_ref.shape[1]
        step = 512 if width % 512 == 0 else BLOCK
        for c0 in range(0, width, step):
            cols = slice(c0, c0 + step)
            part = jnp.dot(c_ref[0], t_ref[:, cols], preferred_element_type=jnp.float32)

            @pl.when(l == 0)
            def _():
                acc_ref[:, cols] = part

            @pl.when(l > 0)
            def _():
                acc_ref[:, cols] += part

        @pl.when(l == pl.num_programs(1) - 1)
        def _():
            for c0 in range(0, width, step):
                cols = slice(c0, c0 + step)
                o_ref[:, cols] = acc_ref[:, cols].astype(o_ref.dtype)


def decode(codes, weights, combine):
    layers, per_owner, rows, _ = codes.shape
    width = weights.shape[2]
    tokens, slot_count = combine.shape[1], combine.shape[2]
    tile = min(tokens, 1024)
    return pl.pallas_call(
        decode_kernel,
        grid=(tokens // tile, layers, per_owner),
        in_specs=[
            pl.BlockSpec((1, 1, rows, BLOCK), lambda t, l, b: (l, b, 0, 0)),
            pl.BlockSpec((1, BLOCK, width), lambda t, l, b: (l, b, 0)),
            pl.BlockSpec((1, tile, slot_count), lambda t, l, b: (l, t, 0)),
        ],
        out_specs=pl.BlockSpec((tile, width), lambda t, l, b: (t, 0)),
        out_shape=jax.ShapeDtypeStruct((tokens, width), jnp.bfloat16),
        scratch_shapes=[
            pltpu.VMEM((slot_count, width), jnp.bfloat16),
            pltpu.VMEM((tile, width), jnp.float32),
        ],
    )(codes, weights, combine)


def pair_slots(ids, per_owner, cap):
    layers = ids.shape[0]
    flat = ids.reshape(layers, -1)
    n = flat.shape[1]
    earlier = jnp.arange(n, dtype=jnp.int32)[None, :] < jnp.arange(n, dtype=jnp.int32)[:, None]
    same = (flat[:, :, None] == flat[:, None, :]) & earlier[None]
    rank = jnp.sum(same.astype(jnp.int32), axis=2)
    return (flat * cap + rank).reshape(ids.shape)


def body(residual, targets, block_ids, encoder_weight, encoder_bias, decoder_weight, decoder_bias):
    layer_index = lax.axis_index("layer")
    tok_index = lax.axis_index("tok")
    layers = lax.axis_size("layer")
    tok_count = lax.axis_size("tok")
    tok_rows = residual.shape[1]
    width = residual.shape[2]
    topk = block_ids.shape[2]
    per_owner = encoder_weight.shape[2] // BLOCK
    blocks = per_owner * tok_count
    cap = max(2, 2 * tok_rows * topk // blocks)
    per_src = per_owner * cap
    tokens = tok_rows * tok_count
    slot_count = per_owner * tok_count * cap

    codes_own = pair_slots(block_ids, per_owner, cap)
    codes_all = lax.all_gather(codes_own, "tok", axis=1, tiled=True)
    local = codes_all.reshape(layers, tok_count, tok_rows, topk) - tok_index * per_src
    src_of = jnp.arange(tok_count, dtype=jnp.int32)[:, None]
    slot_of = jnp.where(
        (local >= 0) & (local < per_src),
        (local // cap) * (tok_count * cap) + src_of[None, :, :, None] * cap + local % cap,
        slot_count,
    ).reshape(layers, tokens, topk)
    onehot = jnp.any(slot_of[..., None] == jnp.arange(slot_count, dtype=jnp.int32), axis=2)

    res_all = lax.all_gather(residual[0], "tok", axis=0, tiled=True)
    own_onehot = lax.dynamic_index_in_dim(onehot, layer_index, 0, keepdims=False).astype(jnp.bfloat16)
    rows = jnp.einsum("tx,td->xd", own_onehot, res_all, preferred_element_type=jnp.float32).astype(jnp.bfloat16)
    codes = encode(rows.reshape(per_owner, tok_count * cap, width), encoder_weight[0], encoder_bias[0].reshape(1, -1))
    gathered = lax.all_gather(codes, "layer", axis=0, tiled=False)

    valid = jnp.arange(layers, dtype=jnp.int32) <= layer_index
    combine = (onehot & valid[:, None, None]).astype(jnp.bfloat16)
    partial = decode(gathered, decoder_weight[0], combine)
    summed = lax.psum_scatter(partial, "tok", scatter_dimension=0, tiled=True)
    recon32 = decoder_bias[0][None, :] + summed.astype(jnp.float32)
    difference = recon32 - targets[0].astype(jnp.float32)
    error = jnp.mean(difference * difference, axis=1)
    return (recon32.astype(jnp.bfloat16)[None], error[None])


def solution(mesh):
    in_specs = (
        P("layer", "tok", None),
        P("layer", "tok", None),
        P(None, "tok", None),
        P("layer", None, "tok"),
        P("layer", "tok"),
        P("layer", None, "tok", None),
        P("layer", None),
    )
    out_specs = (P("layer", "tok", None), P("layer", "tok"))
    return jax.shard_map(body, mesh=mesh, in_specs=in_specs, out_specs=out_specs, check_vma=False)
```

```python
import math

import jax
import jax.numpy as jnp
from jax import lax
from jax.experimental import pallas as pl
from jax.sharding import PartitionSpec as P

BLOCK = 128


def encode_kernel(rows_ref, w_ref, b_ref, o_ref):
    group = rows_ref.shape[0]
    for i in range(group):
        cols = slice(i * BLOCK, (i + 1) * BLOCK)
        acc = jnp.dot(rows_ref[i], w_ref[:, cols], preferred_element_type=jnp.float32)
        acc = acc + b_ref[:, cols]
        o_ref[i] = jnp.maximum(acc, 0.0).astype(o_ref.dtype)


def encode(rows, weight, bias):
    per_owner, capacity, width = rows.shape
    group = math.gcd(per_owner, 4)
    return pl.pallas_call(
        encode_kernel,
        grid=(per_owner // group,),
        in_specs=[
            pl.BlockSpec((group, capacity, width), lambda g: (g, 0, 0)),
            pl.BlockSpec((width, group * BLOCK), lambda g: (0, g)),
            pl.BlockSpec((1, group * BLOCK), lambda g: (0, g)),
        ],
        out_specs=pl.BlockSpec((group, capacity, BLOCK), lambda g: (g, 0, 0)),
        out_shape=jax.ShapeDtypeStruct((per_owner, capacity, BLOCK), jnp.bfloat16),
    )(rows, weight, bias)


def pair_slots(ids, per_owner, cap):
    layers = ids.shape[0]
    flat = ids.reshape(layers, -1)
    n = flat.shape[1]
    earlier = jnp.arange(n, dtype=jnp.int32)[None, :] < jnp.arange(n, dtype=jnp.int32)[:, None]
    same = (flat[:, :, None] == flat[:, None, :]) & earlier[None]
    rank = jnp.sum(same.astype(jnp.int32), axis=2)
    return (flat * cap + rank).reshape(ids.shape)


def body(residual, targets, block_ids, encoder_weight, encoder_bias, decoder_weight, decoder_bias):
    layer_index = lax.axis_index("layer")
    tok_index = lax.axis_index("tok")
    layers = lax.axis_size("layer")
    tok_count = lax.axis_size("tok")
    tok_rows = residual.shape[1]
    width = residual.shape[2]
    topk = block_ids.shape[2]
    per_owner = encoder_weight.shape[2] // BLOCK
    blocks = per_owner * tok_count
    cap = max(2, 2 * tok_rows * topk // blocks)
    per_src = per_owner * cap
    tokens = tok_rows * tok_count
    slot_count = per_owner * tok_count * cap

    codes_own = pair_slots(block_ids, per_owner, cap)
    codes_all = lax.all_gather(codes_own, "tok", axis=1, tiled=True)
    local = codes_all.reshape(layers, tok_count, tok_rows, topk) - tok_index * per_src
    src_of = jnp.arange(tok_count, dtype=jnp.int32)[:, None]
    slot_of = jnp.where(
        (local >= 0) & (local < per_src),
        (local // cap) * (tok_count * cap) + src_of[None, :, :, None] * cap + local % cap,
        slot_count,
    ).reshape(layers, tokens, topk)
    onehot = jnp.any(slot_of[..., None] == jnp.arange(slot_count, dtype=jnp.int32), axis=2)

    res_all = lax.all_gather(residual[0], "tok", axis=0, tiled=True)
    own_onehot = lax.dynamic_index_in_dim(onehot, layer_index, 0, keepdims=False).astype(jnp.bfloat16)
    rows = jnp.einsum("tx,td->xd", own_onehot, res_all, preferred_element_type=jnp.float32).astype(jnp.bfloat16)
    codes = encode(rows.reshape(per_owner, tok_count * cap, width), encoder_weight[0], encoder_bias[0].reshape(1, -1))
    gathered = lax.all_gather(codes, "layer", axis=0, tiled=False)

    valid = jnp.arange(layers, dtype=jnp.int32) <= layer_index
    combine = (onehot & valid[:, None, None]).astype(jnp.bfloat16)
    terms = jnp.einsum(
        "lbxe,lbed->lbxd",
        gathered,
        decoder_weight[0].reshape(layers, per_owner, BLOCK, width),
        preferred_element_type=jnp.float32,
    ).astype(jnp.bfloat16)
    partial = jnp.einsum(
        "ltx,lxd->td",
        combine,
        terms.reshape(layers, slot_count, width),
        preferred_element_type=jnp.float32,
    ).astype(jnp.bfloat16)
    summed = lax.psum_scatter(partial, "tok", scatter_dimension=0, tiled=True)
    recon32 = decoder_bias[0][None, :] + summed.astype(jnp.float32)
    difference = recon32 - targets[0].astype(jnp.float32)
    error = jnp.mean(difference * difference, axis=1)
    return (recon32.astype(jnp.bfloat16)[None], error[None])


def solution(mesh):
    in_specs = (
        P("layer", "tok", None),
        P("layer", "tok", None),
        P(None, "tok", None),
        P("layer", None, "tok"),
        P("layer", "tok"),
        P("layer", None, "tok", None),
        P("layer", None),
    )
    out_specs = (P("layer", "tok", None), P("layer", "tok"))
    return jax.shard_map(body, mesh=mesh, in_specs=in_specs, out_specs=out_specs, check_vma=False)
```

```python
import math

import jax
import jax.numpy as jnp
from jax import lax
from jax.experimental import pallas as pl
from jax.sharding import PartitionSpec as P

BLOCK = 128


def encode_kernel(rows_ref, w_ref, b_ref, o_ref):
    group = rows_ref.shape[0]
    for i in range(group):
        cols = slice(i * BLOCK, (i + 1) * BLOCK)
        acc = jnp.dot(rows_ref[i], w_ref[:, cols], preferred_element_type=jnp.float32)
        acc = acc + b_ref[:, cols]
        o_ref[i] = jnp.maximum(acc, 0.0).astype(o_ref.dtype)


def encode(rows, weight, bias):
    per_owner, capacity, width = rows.shape
    group = math.gcd(per_owner, 4)
    return pl.pallas_call(
        encode_kernel,
        grid=(per_owner // group,),
        in_specs=[
            pl.BlockSpec((group, capacity, width), lambda g: (g, 0, 0)),
            pl.BlockSpec((width, group * BLOCK), lambda g: (0, g)),
            pl.BlockSpec((1, group * BLOCK), lambda g: (0, g)),
        ],
        out_specs=pl.BlockSpec((group, capacity, BLOCK), lambda g: (g, 0, 0)),
        out_shape=jax.ShapeDtypeStruct((per_owner, capacity, BLOCK), jnp.bfloat16),
    )(rows, weight, bias)


def pair_slots(ids, per_owner, cap):
    layers = ids.shape[0]
    flat = ids.reshape(layers, -1)
    n = flat.shape[1]
    earlier = jnp.arange(n, dtype=jnp.int32)[None, :] < jnp.arange(n, dtype=jnp.int32)[:, None]
    same = (flat[:, :, None] == flat[:, None, :]) & earlier[None]
    rank = jnp.sum(same.astype(jnp.int32), axis=2)
    return (flat * cap + rank).reshape(ids.shape)


def body(residual, targets, block_ids, encoder_weight, encoder_bias, decoder_weight, decoder_bias):
    layer_index = lax.axis_index("layer")
    tok_index = lax.axis_index("tok")
    layers = lax.axis_size("layer")
    tok_count = lax.axis_size("tok")
    tok_rows = residual.shape[1]
    width = residual.shape[2]
    topk = block_ids.shape[2]
    per_owner = encoder_weight.shape[2] // BLOCK
    blocks = per_owner * tok_count
    cap = max(2, 2 * tok_rows * topk // blocks)
    per_src = per_owner * cap
    tokens = tok_rows * tok_count
    slot_count = per_owner * tok_count * cap

    codes_own = pair_slots(block_ids, per_owner, cap)
    codes_all = lax.all_gather(codes_own, "tok", axis=1, tiled=True)
    local = codes_all.reshape(layers, tok_count, tok_rows, topk) - tok_index * per_src
    src_of = jnp.arange(tok_count, dtype=jnp.int32)[:, None]
    slot_of = jnp.where(
        (local >= 0) & (local < per_src),
        (local // cap) * (tok_count * cap) + src_of[None, :, :, None] * cap + local % cap,
        slot_count,
    ).reshape(layers, tokens, topk)
    onehot = jnp.any(slot_of[..., None] == jnp.arange(slot_count, dtype=jnp.int32), axis=2)

    res_all = lax.all_gather(residual[0], "tok", axis=0, tiled=True)
    own_onehot = lax.dynamic_index_in_dim(onehot, layer_index, 0, keepdims=False).astype(jnp.bfloat16)
    rows = jnp.einsum("tx,td->xd", own_onehot, res_all, preferred_element_type=jnp.float32).astype(jnp.bfloat16)
    codes = encode(rows.reshape(per_owner, tok_count * cap, width), encoder_weight[0], encoder_bias[0].reshape(1, -1))
    received = [codes] + [
        lax.ppermute(codes, "layer", [(i, i + shift) for i in range(layers - shift)])
        for shift in range(1, layers)
    ]
    shifts = (layer_index - jnp.arange(layers, dtype=jnp.int32)) % layers
    gathered = jnp.take(jnp.stack(received), shifts, axis=0)

    valid = jnp.arange(layers, dtype=jnp.int32) <= layer_index
    terms = jnp.einsum(
        "lbxe,lbed->lbxd",
        gathered,
        decoder_weight[0].reshape(layers, per_owner, BLOCK, width),
        preferred_element_type=jnp.float32,
    ).astype(jnp.bfloat16)
    halves = 2 if (tok_count % 2 == 0 and (tok_count // 2) * cap % 16 == 0) else 1
    rows_half = tok_count * cap // halves
    used = (slot_of < slot_count) & valid[:, None, None]
    block_hit = (slot_of // (tok_count * cap))[..., None] == jnp.arange(per_owner, dtype=jnp.int32)
    row_hit = (slot_of % rows_half)[..., None] == jnp.arange(rows_half, dtype=jnp.int32)
    combine = jnp.any(block_hit[..., :, None] & row_hit[..., None, :] & used[..., None, None], axis=2)
    combine = combine.astype(jnp.bfloat16).reshape(layers, halves, tokens // halves, per_owner, rows_half)
    partial = jnp.einsum(
        "lgtbx,lbgxd->gtd",
        combine,
        terms.reshape(layers, per_owner, halves, rows_half, width),
        preferred_element_type=jnp.float32,
    ).reshape(tokens, width).astype(jnp.bfloat16)
    summed = lax.psum_scatter(partial, "tok", scatter_dimension=0, tiled=True)
    recon32 = decoder_bias[0][None, :] + summed.astype(jnp.float32)
    difference = recon32 - targets[0].astype(jnp.float32)
    error = jnp.mean(difference * difference, axis=1)
    return (recon32.astype(jnp.bfloat16)[None], error[None])


def solution(mesh):
    in_specs = (
        P("layer", "tok", None),
        P("layer", "tok", None),
        P(None, "tok", None),
        P("layer", None, "tok"),
        P("layer", "tok"),
        P("layer", None, "tok", None),
        P("layer", None),
    )
    out_specs = (P("layer", "tok", None), P("layer", "tok"))
    return jax.shard_map(body, mesh=mesh, in_specs=in_specs, out_specs=out_specs, check_vma=False)
```

```python
import math

import jax
import jax.numpy as jnp
from jax import lax
from jax.experimental import pallas as pl
from jax.sharding import PartitionSpec as P

BLOCK = 128


def encode_kernel(rows_ref, w_ref, b_ref, o_ref):
    group = rows_ref.shape[0]
    for i in range(group):
        cols = slice(i * BLOCK, (i + 1) * BLOCK)
        acc = jnp.dot(rows_ref[i], w_ref[:, cols], preferred_element_type=jnp.float32)
        acc = acc + b_ref[:, cols]
        o_ref[i] = jnp.maximum(acc, 0.0).astype(o_ref.dtype)


def encode(rows, weight, bias):
    per_owner, capacity, width = rows.shape
    group = math.gcd(per_owner, 4)
    return pl.pallas_call(
        encode_kernel,
        grid=(per_owner // group,),
        in_specs=[
            pl.BlockSpec((group, capacity, width), lambda g: (g, 0, 0)),
            pl.BlockSpec((width, group * BLOCK), lambda g: (0, g)),
            pl.BlockSpec((1, group * BLOCK), lambda g: (0, g)),
        ],
        out_specs=pl.BlockSpec((group, capacity, BLOCK), lambda g: (g, 0, 0)),
        out_shape=jax.ShapeDtypeStruct((per_owner, capacity, BLOCK), jnp.bfloat16),
    )(rows, weight, bias)


def line_reduce_scatter(partial, tok_index, tok_count):
    chips = tok_count // 2
    rows = partial.shape[0] // tok_count
    chip = tok_index // 2
    core = tok_index % 2
    blocks = partial.reshape(chips, 2, rows, partial.shape[1])
    mine = lax.dynamic_index_in_dim(blocks, core, 1, keepdims=False)
    other = lax.dynamic_index_in_dim(blocks, 1 - core, 1, keepdims=False).astype(jnp.bfloat16)
    swapped = lax.ppermute(other, "tok", [(i, i ^ 1) for i in range(tok_count)])
    q = mine + swapped.astype(jnp.float32)
    right = jnp.zeros(q.shape[1:], jnp.float32)
    left = jnp.zeros(q.shape[1:], jnp.float32)
    for r in range(1, chips):
        d = jnp.clip(chip + chips - r, 0, chips - 1)
        send = (lax.dynamic_index_in_dim(q, d, 0, keepdims=False) + right).astype(jnp.bfloat16)
        e = jnp.clip(chip - (chips - r), 0, chips - 1)
        send_left = (lax.dynamic_index_in_dim(q, e, 0, keepdims=False) + left).astype(jnp.bfloat16)
        right = lax.ppermute(
            send, "tok", [(2 * c + k, 2 * (c + 1) + k) for c in range(r) for k in range(2)]
        ).astype(jnp.float32)
        left = lax.ppermute(
            send_left, "tok", [(2 * c + k, 2 * (c - 1) + k) for c in range(chips - r, chips) for k in range(2)]
        ).astype(jnp.float32)
    return lax.dynamic_index_in_dim(q, chip, 0, keepdims=False) + right + left


def pair_slots(ids, per_owner, cap):
    layers = ids.shape[0]
    flat = ids.reshape(layers, -1)
    n = flat.shape[1]
    earlier = jnp.arange(n, dtype=jnp.int32)[None, :] < jnp.arange(n, dtype=jnp.int32)[:, None]
    same = (flat[:, :, None] == flat[:, None, :]) & earlier[None]
    rank = jnp.sum(same.astype(jnp.int32), axis=2)
    return (flat * cap + rank).reshape(ids.shape)


def body(residual, targets, block_ids, encoder_weight, encoder_bias, decoder_weight, decoder_bias):
    layer_index = lax.axis_index("layer")
    tok_index = lax.axis_index("tok")
    layers = lax.axis_size("layer")
    tok_count = lax.axis_size("tok")
    tok_rows = residual.shape[1]
    width = residual.shape[2]
    topk = block_ids.shape[2]
    per_owner = encoder_weight.shape[2] // BLOCK
    blocks = per_owner * tok_count
    cap = max(2, 2 * tok_rows * topk // blocks)
    per_src = per_owner * cap
    tokens = tok_rows * tok_count
    slot_count = per_owner * tok_count * cap

    codes_own = pair_slots(block_ids, per_owner, cap)
    codes_all = lax.all_gather(codes_own, "tok", axis=1, tiled=True)
    local = codes_all.reshape(layers, tok_count, tok_rows, topk) - tok_index * per_src
    src_of = jnp.arange(tok_count, dtype=jnp.int32)[:, None]
    slot_of = jnp.where(
        (local >= 0) & (local < per_src),
        (local // cap) * (tok_count * cap) + src_of[None, :, :, None] * cap + local % cap,
        slot_count,
    ).reshape(layers, tokens, topk)
    onehot = jnp.any(slot_of[..., None] == jnp.arange(slot_count, dtype=jnp.int32), axis=2)

    res_all = lax.all_gather(residual[0], "tok", axis=0, tiled=True)
    own_onehot = lax.dynamic_index_in_dim(onehot, layer_index, 0, keepdims=False).astype(jnp.bfloat16)
    rows = jnp.einsum("tx,td->xd", own_onehot, res_all, preferred_element_type=jnp.float32).astype(jnp.bfloat16)
    codes = encode(rows.reshape(per_owner, tok_count * cap, width), encoder_weight[0], encoder_bias[0].reshape(1, -1))
    received = [codes] + [
        lax.ppermute(codes, "layer", [(i, i + shift) for i in range(layers - shift)])
        for shift in range(1, layers)
    ]
    shifts = (layer_index - jnp.arange(layers, dtype=jnp.int32)) % layers
    gathered = jnp.take(jnp.stack(received), shifts, axis=0)

    valid = jnp.arange(layers, dtype=jnp.int32) <= layer_index
    terms = jnp.einsum(
        "lbxe,lbed->lbxd",
        gathered,
        decoder_weight[0].reshape(layers, per_owner, BLOCK, width),
        preferred_element_type=jnp.float32,
    ).astype(jnp.bfloat16)
    halves = 2 if (tok_count % 2 == 0 and (tok_count // 2) * cap % 16 == 0) else 1
    rows_half = tok_count * cap // halves
    used = (slot_of < slot_count) & valid[:, None, None]
    block_hit = (slot_of // (tok_count * cap))[..., None] == jnp.arange(per_owner, dtype=jnp.int32)
    row_hit = (slot_of % rows_half)[..., None] == jnp.arange(rows_half, dtype=jnp.int32)
    combine = jnp.any(block_hit[..., :, None] & row_hit[..., None, :] & used[..., None, None], axis=2)
    combine = combine.astype(jnp.bfloat16).reshape(layers, halves, tokens // halves, per_owner, rows_half)
    partial = jnp.einsum(
        "lgtbx,lbgxd->gtd",
        combine,
        terms.reshape(layers, per_owner, halves, rows_half, width),
        preferred_element_type=jnp.float32,
    ).reshape(tokens, width)
    if tok_count % 2 == 0 and tok_count <= 8:
        summed = line_reduce_scatter(partial, tok_index, tok_count)
    else:
        summed = lax.psum_scatter(partial.astype(jnp.bfloat16), "tok", scatter_dimension=0, tiled=True)
    recon32 = decoder_bias[0][None, :] + summed.astype(jnp.float32)
    difference = recon32 - targets[0].astype(jnp.float32)
    error = jnp.mean(difference * difference, axis=1)
    return (recon32.astype(jnp.bfloat16)[None], error[None])


def solution(mesh):
    in_specs = (
        P("layer", "tok", None),
        P("layer", "tok", None),
        P(None, "tok", None),
        P("layer", None, "tok"),
        P("layer", "tok"),
        P("layer", None, "tok", None),
        P("layer", None),
    )
    out_specs = (P("layer", "tok", None), P("layer", "tok"))
    return jax.shard_map(body, mesh=mesh, in_specs=in_specs, out_specs=out_specs, check_vma=False)
```

```python
import math

import jax
import jax.numpy as jnp
from jax import lax
from jax.experimental import pallas as pl
from jax.sharding import PartitionSpec as P

BLOCK = 128


def encode_kernel(rows_ref, w_ref, b_ref, o_ref):
    halves, group, rows_half, width = rows_ref.shape
    for i in range(group):
        cols = slice(i * BLOCK, (i + 1) * BLOCK)
        rows = rows_ref[:, i].reshape(halves * rows_half, width)
        acc = jnp.dot(rows, w_ref[:, cols], preferred_element_type=jnp.float32)
        acc = acc + b_ref[:, cols]
        o_ref[i] = jnp.maximum(acc, 0.0).astype(o_ref.dtype)


def encode(rows, weight, bias):
    halves, per_owner, rows_half, width = rows.shape
    group = math.gcd(per_owner, 4)
    return pl.pallas_call(
        encode_kernel,
        grid=(per_owner // group,),
        in_specs=[
            pl.BlockSpec((halves, group, rows_half, width), lambda g: (0, g, 0, 0)),
            pl.BlockSpec((width, group * BLOCK), lambda g: (0, g)),
            pl.BlockSpec((1, group * BLOCK), lambda g: (0, g)),
        ],
        out_specs=pl.BlockSpec((group, halves * rows_half, BLOCK), lambda g: (g, 0, 0)),
        out_shape=jax.ShapeDtypeStruct((per_owner, halves * rows_half, BLOCK), jnp.bfloat16),
    )(rows, weight, bias)


def pair_slots(ids, per_owner, cap):
    layers = ids.shape[0]
    flat = ids.reshape(layers, -1)
    n = flat.shape[1]
    earlier = jnp.arange(n, dtype=jnp.int32)[None, :] < jnp.arange(n, dtype=jnp.int32)[:, None]
    same = (flat[:, :, None] == flat[:, None, :]) & earlier[None]
    rank = jnp.sum(same.astype(jnp.int32), axis=2)
    return (flat * cap + rank).reshape(ids.shape)


def body(residual, targets, block_ids, encoder_weight, encoder_bias, decoder_weight, decoder_bias):
    layer_index = lax.axis_index("layer")
    tok_index = lax.axis_index("tok")
    layers = lax.axis_size("layer")
    tok_count = lax.axis_size("tok")
    tok_rows = residual.shape[1]
    width = residual.shape[2]
    topk = block_ids.shape[2]
    per_owner = encoder_weight.shape[2] // BLOCK
    blocks = per_owner * tok_count
    cap = max(2, 2 * tok_rows * topk // blocks)
    per_src = per_owner * cap
    tokens = tok_rows * tok_count
    slot_count = per_owner * tok_count * cap

    codes_own = pair_slots(block_ids, per_owner, cap)
    codes_all = lax.all_gather(codes_own, "tok", axis=1, tiled=True)
    local = codes_all.reshape(layers, tok_count, tok_rows, topk) - tok_index * per_src
    src_of = jnp.arange(tok_count, dtype=jnp.int32)[:, None]
    slot_of = jnp.where(
        (local >= 0) & (local < per_src),
        (local // cap) * (tok_count * cap) + src_of[None, :, :, None] * cap + local % cap,
        slot_count,
    ).reshape(layers, tokens, topk)
    halves = 2 if (tok_count % 2 == 0 and (tok_count // 2) * cap % 16 == 0) else 1
    rows_half = tok_count * cap // halves
    block_hit = (slot_of // (tok_count * cap))[..., None] == jnp.arange(per_owner, dtype=jnp.int32)
    row_hit = (slot_of % rows_half)[..., None] == jnp.arange(rows_half, dtype=jnp.int32)
    used = slot_of < slot_count
    hits = jnp.any(block_hit[..., :, None] & row_hit[..., None, :] & used[..., None, None], axis=2)

    res_all = lax.all_gather(residual[0], "tok", axis=0, tiled=True)
    own_hits = lax.dynamic_index_in_dim(hits, layer_index, 0, keepdims=False).astype(jnp.bfloat16)
    rows = jnp.einsum(
        "gtbx,gtd->gbxd",
        own_hits.reshape(halves, tokens // halves, per_owner, rows_half),
        res_all.reshape(halves, tokens // halves, width),
        preferred_element_type=jnp.float32,
    ).astype(jnp.bfloat16)
    codes = encode(rows, encoder_weight[0], encoder_bias[0].reshape(1, -1))
    received = [codes] + [
        lax.ppermute(codes, "layer", [(i, i + shift) for i in range(layers - shift)])
        for shift in range(1, layers)
    ]
    shifts = (layer_index - jnp.arange(layers, dtype=jnp.int32)) % layers
    gathered = jnp.take(jnp.stack(received), shifts, axis=0)

    valid = jnp.arange(layers, dtype=jnp.int32) <= layer_index
    terms = jnp.einsum(
        "lbxe,lbed->lbxd",
        gathered,
        decoder_weight[0].reshape(layers, per_owner, BLOCK, width),
        preferred_element_type=jnp.float32,
    ).astype(jnp.bfloat16)
    combine = (hits & valid[:, None, None, None]).astype(jnp.bfloat16)
    combine = combine.reshape(layers, halves, tokens // halves, per_owner, rows_half)
    partial = jnp.einsum(
        "lgtbx,lbgxd->gtd",
        combine,
        terms.reshape(layers, per_owner, halves, rows_half, width),
        preferred_element_type=jnp.float32,
    ).reshape(tokens, width).astype(jnp.bfloat16)
    summed = lax.psum_scatter(partial, "tok", scatter_dimension=0, tiled=True)
    recon32 = decoder_bias[0][None, :] + summed.astype(jnp.float32)
    difference = recon32 - targets[0].astype(jnp.float32)
    error = jnp.mean(difference * difference, axis=1)
    return (recon32.astype(jnp.bfloat16)[None], error[None])


def solution(mesh):
    in_specs = (
        P("layer", "tok", None),
        P("layer", "tok", None),
        P(None, "tok", None),
        P("layer", None, "tok"),
        P("layer", "tok"),
        P("layer", None, "tok", None),
        P("layer", None),
    )
    out_specs = (P("layer", "tok", None), P("layer", "tok"))
    return jax.shard_map(body, mesh=mesh, in_specs=in_specs, out_specs=out_specs, check_vma=False)
```

```python
import math

import jax
import jax.numpy as jnp
from jax import lax
from jax.experimental import pallas as pl
from jax.sharding import PartitionSpec as P

BLOCK = 128


def encode_kernel(rows_ref, w_ref, b_ref, o_ref):
    halves, group, rows_half, width = rows_ref.shape
    for i in range(group):
        cols = slice(i * BLOCK, (i + 1) * BLOCK)
        rows = rows_ref[:, i].reshape(halves * rows_half, width)
        acc = jnp.dot(rows, w_ref[:, cols], preferred_element_type=jnp.float32)
        acc = acc + b_ref[:, cols]
        o_ref[i] = jnp.maximum(acc, 0.0).astype(o_ref.dtype)


def encode(rows, weight, bias):
    halves, per_owner, rows_half, width = rows.shape
    group = math.gcd(per_owner, 4)
    return pl.pallas_call(
        encode_kernel,
        grid=(per_owner // group,),
        in_specs=[
            pl.BlockSpec((halves, group, rows_half, width), lambda g: (0, g, 0, 0)),
            pl.BlockSpec((width, group * BLOCK), lambda g: (0, g)),
            pl.BlockSpec((1, group * BLOCK), lambda g: (0, g)),
        ],
        out_specs=pl.BlockSpec((group, halves * rows_half, BLOCK), lambda g: (g, 0, 0)),
        out_shape=jax.ShapeDtypeStruct((per_owner, halves * rows_half, BLOCK), jnp.bfloat16),
    )(rows, weight, bias)


def pair_slots(ids, per_owner, cap):
    layers = ids.shape[0]
    flat = ids.reshape(layers, -1)
    n = flat.shape[1]
    earlier = jnp.arange(n, dtype=jnp.int32)[None, :] < jnp.arange(n, dtype=jnp.int32)[:, None]
    same = (flat[:, :, None] == flat[:, None, :]) & earlier[None]
    rank = jnp.sum(same.astype(jnp.int32), axis=2)
    return (flat * cap + rank).reshape(ids.shape)


def body(residual, targets, block_ids, encoder_weight, encoder_bias, decoder_weight, decoder_bias):
    layer_index = lax.axis_index("layer")
    tok_index = lax.axis_index("tok")
    layers = lax.axis_size("layer")
    tok_count = lax.axis_size("tok")
    tok_rows = residual.shape[1]
    width = residual.shape[2]
    topk = block_ids.shape[2]
    per_owner = encoder_weight.shape[2] // BLOCK
    blocks = per_owner * tok_count
    cap = max(2, 2 * tok_rows * topk // blocks)
    per_src = per_owner * cap
    tokens = tok_rows * tok_count
    slot_count = per_owner * tok_count * cap

    codes_own = pair_slots(block_ids, per_owner, cap)
    codes_all = lax.all_gather(codes_own, "tok", axis=1, tiled=True)
    local = codes_all.reshape(layers, tok_count, tok_rows, topk) - tok_index * per_src
    src_of = jnp.arange(tok_count, dtype=jnp.int32)[:, None]
    slot_of = jnp.where(
        (local >= 0) & (local < per_src),
        (local // cap) * (tok_count * cap) + src_of[None, :, :, None] * cap + local % cap,
        slot_count,
    ).reshape(layers, tokens, topk)
    halves = 2 if (tok_count % 2 == 0 and (tok_count // 2) * cap % 16 == 0) else 1
    rows_half = tok_count * cap // halves
    block_hit = (slot_of // (tok_count * cap))[..., None] == jnp.arange(per_owner, dtype=jnp.int32)
    row_hit = (slot_of % rows_half)[..., None] == jnp.arange(rows_half, dtype=jnp.int32)
    used = slot_of < slot_count
    hits = jnp.any(block_hit[..., :, None] & row_hit[..., None, :] & used[..., None, None], axis=2)

    res_all = lax.all_gather(residual[0], "tok", axis=0, tiled=True)
    own_hits = lax.dynamic_index_in_dim(hits, layer_index, 0, keepdims=False).astype(jnp.bfloat16)
    rows = jnp.einsum(
        "gtbx,gtd->gbxd",
        own_hits.reshape(halves, tokens // halves, per_owner, rows_half),
        res_all.reshape(halves, tokens // halves, width),
        preferred_element_type=jnp.float32,
    ).astype(jnp.bfloat16)
    codes = encode(rows, encoder_weight[0], encoder_bias[0].reshape(1, -1))
    received = [codes] + [
        lax.ppermute(codes, "layer", [(i, i + shift) for i in range(layers - shift)])
        for shift in range(1, layers)
    ]
    shifts = (layer_index - jnp.arange(layers, dtype=jnp.int32)) % layers
    gathered = jnp.take(jnp.stack(received), shifts, axis=0)

    valid = jnp.arange(layers, dtype=jnp.int32) <= layer_index
    combine = (hits & valid[:, None, None, None]).astype(jnp.bfloat16)
    combine = combine.reshape(layers, halves, tokens // halves, per_owner, rows_half)
    weights = decoder_weight[0].reshape(layers, per_owner, BLOCK, width)
    chunks = 2 if width % (2 * BLOCK) == 0 else 1
    step = width // chunks
    pieces = []
    for c in range(chunks):
        terms = jnp.einsum(
            "lbxe,lbed->lbxd",
            gathered,
            weights[..., c * step:(c + 1) * step],
            preferred_element_type=jnp.float32,
        ).astype(jnp.bfloat16)
        partial = jnp.einsum(
            "lgtbx,lbgxd->gtd",
            combine,
            terms.reshape(layers, per_owner, halves, rows_half, step),
            preferred_element_type=jnp.float32,
        ).reshape(tokens, step).astype(jnp.bfloat16)
        pieces.append(lax.psum_scatter(partial, "tok", scatter_dimension=0, tiled=True))
    summed = jnp.concatenate(pieces, axis=1)
    recon32 = decoder_bias[0][None, :] + summed.astype(jnp.float32)
    difference = recon32 - targets[0].astype(jnp.float32)
    error = jnp.mean(difference * difference, axis=1)
    return (recon32.astype(jnp.bfloat16)[None], error[None])


def solution(mesh):
    in_specs = (
        P("layer", "tok", None),
        P("layer", "tok", None),
        P(None, "tok", None),
        P("layer", None, "tok"),
        P("layer", "tok"),
        P("layer", None, "tok", None),
        P("layer", None),
    )
    out_specs = (P("layer", "tok", None), P("layer", "tok"))
    return jax.shard_map(body, mesh=mesh, in_specs=in_specs, out_specs=out_specs, check_vma=False)
```

```python
import math

import jax
import jax.numpy as jnp
from jax import lax
from jax.experimental import pallas as pl
from jax.sharding import PartitionSpec as P

BLOCK = 128


def encode_kernel(rows_ref, w_ref, b_ref, o_ref):
    halves, group, rows_half, width = rows_ref.shape
    for i in range(group):
        cols = slice(i * BLOCK, (i + 1) * BLOCK)
        rows = rows_ref[:, i].reshape(halves * rows_half, width)
        acc = jnp.dot(rows, w_ref[:, cols], preferred_element_type=jnp.float32)
        acc = acc + b_ref[:, cols]
        o_ref[i] = jnp.maximum(acc, 0.0).astype(o_ref.dtype)


def encode(rows, weight, bias):
    halves, per_owner, rows_half, width = rows.shape
    group = math.gcd(per_owner, 4)
    return pl.pallas_call(
        encode_kernel,
        grid=(per_owner // group,),
        in_specs=[
            pl.BlockSpec((halves, group, rows_half, width), lambda g: (0, g, 0, 0)),
            pl.BlockSpec((width, group * BLOCK), lambda g: (0, g)),
            pl.BlockSpec((1, group * BLOCK), lambda g: (0, g)),
        ],
        out_specs=pl.BlockSpec((group, halves * rows_half, BLOCK), lambda g: (g, 0, 0)),
        out_shape=jax.ShapeDtypeStruct((per_owner, halves * rows_half, BLOCK), jnp.bfloat16),
    )(rows, weight, bias)


def pair_slots(ids, per_owner, cap):
    layers = ids.shape[0]
    flat = ids.reshape(layers, -1)
    n = flat.shape[1]
    earlier = jnp.arange(n, dtype=jnp.int32)[None, :] < jnp.arange(n, dtype=jnp.int32)[:, None]
    same = (flat[:, :, None] == flat[:, None, :]) & earlier[None]
    rank = jnp.sum(same.astype(jnp.int32), axis=2)
    return (flat * cap + rank).reshape(ids.shape)


def body(residual, targets, block_ids, encoder_weight, encoder_bias, decoder_weight, decoder_bias):
    layer_index = lax.axis_index("layer")
    tok_index = lax.axis_index("tok")
    layers = lax.axis_size("layer")
    tok_count = lax.axis_size("tok")
    tok_rows = residual.shape[1]
    width = residual.shape[2]
    topk = block_ids.shape[2]
    per_owner = encoder_weight.shape[2] // BLOCK
    blocks = per_owner * tok_count
    cap = max(2, 2 * tok_rows * topk // blocks)
    per_src = per_owner * cap
    tokens = tok_rows * tok_count
    slot_count = per_owner * tok_count * cap

    codes_own = pair_slots(block_ids, per_owner, cap)
    codes_all = lax.all_gather(codes_own, "tok", axis=1, tiled=True)
    local = codes_all.reshape(layers, tok_count, tok_rows, topk) - tok_index * per_src
    src_of = jnp.arange(tok_count, dtype=jnp.int32)[:, None]
    slot_of = jnp.where(
        (local >= 0) & (local < per_src),
        (local // cap) * (tok_count * cap) + src_of[None, :, :, None] * cap + local % cap,
        slot_count,
    ).reshape(layers, tokens, topk)
    halves = 2 if (tok_count % 2 == 0 and (tok_count // 2) * cap % 16 == 0) else 1
    rows_half = tok_count * cap // halves
    block_hit = (slot_of // (tok_count * cap))[..., None] == jnp.arange(per_owner, dtype=jnp.int32)
    row_hit = (slot_of % rows_half)[..., None] == jnp.arange(rows_half, dtype=jnp.int32)
    used = slot_of < slot_count
    hits = jnp.any(block_hit[..., :, None] & row_hit[..., None, :] & used[..., None, None], axis=2)

    res_all = lax.all_gather(residual[0], "tok", axis=0, tiled=True)
    own_hits = lax.dynamic_index_in_dim(hits, layer_index, 0, keepdims=False).astype(jnp.bfloat16)
    rows = jnp.einsum(
        "gtbx,gtd->gbxd",
        own_hits.reshape(halves, tokens // halves, per_owner, rows_half),
        res_all.reshape(halves, tokens // halves, width),
        preferred_element_type=jnp.float32,
    ).astype(jnp.bfloat16)
    codes = encode(rows, encoder_weight[0], encoder_bias[0].reshape(1, -1))
    received = [codes] + [
        lax.ppermute(codes, "layer", [(i, i + shift) for i in range(layers - shift)])
        for shift in range(1, layers)
    ]
    shifts = (layer_index - jnp.arange(layers, dtype=jnp.int32)) % layers
    gathered = jnp.take(jnp.stack(received), shifts, axis=0)

    valid = jnp.arange(layers, dtype=jnp.int32) <= layer_index
    combine = (hits & valid[:, None, None, None]).astype(jnp.bfloat16)
    combine = combine.reshape(layers, halves, tokens // halves, per_owner, rows_half)
    weights = decoder_weight[0].reshape(layers, per_owner, BLOCK, width)
    cut = (width // BLOCK) * 2 // 7 * BLOCK if width % BLOCK == 0 else 0
    bounds = [0, cut, width] if 0 < cut < width else [0, width]
    pieces = []
    chunk_codes = gathered
    for lo, hi in zip(bounds[:-1], bounds[1:]):
        terms = jnp.einsum(
            "lbxe,lbed->lbxd",
            chunk_codes,
            weights[..., lo:hi],
            preferred_element_type=jnp.float32,
        ).astype(jnp.bfloat16)
        partial = jnp.einsum(
            "lgtbx,lbgxd->gtd",
            combine,
            terms.reshape(layers, per_owner, halves, rows_half, hi - lo),
            preferred_element_type=jnp.float32,
        ).reshape(tokens, hi - lo).astype(jnp.bfloat16)
        chunk_codes, partial = lax.optimization_barrier((chunk_codes, partial))
        pieces.append(lax.psum_scatter(partial, "tok", scatter_dimension=0, tiled=True))
    summed = jnp.concatenate(pieces, axis=1)
    recon32 = decoder_bias[0][None, :] + summed.astype(jnp.float32)
    difference = recon32 - targets[0].astype(jnp.float32)
    error = jnp.mean(difference * difference, axis=1)
    return (recon32.astype(jnp.bfloat16)[None], error[None])


def solution(mesh):
    in_specs = (
        P("layer", "tok", None),
        P("layer", "tok", None),
        P(None, "tok", None),
        P("layer", None, "tok"),
        P("layer", "tok"),
        P("layer", None, "tok", None),
        P("layer", None),
    )
    out_specs = (P("layer", "tok", None), P("layer", "tok"))
    return jax.shard_map(body, mesh=mesh, in_specs=in_specs, out_specs=out_specs, check_vma=False)
```

```python
import math

import jax
import jax.numpy as jnp
from jax import lax
from jax.experimental import pallas as pl
from jax.sharding import PartitionSpec as P

BLOCK = 128


def encode_kernel(rows_ref, w_ref, b_ref, o_ref):
    halves, group, rows_half, width = rows_ref.shape
    for i in range(group):
        cols = slice(i * BLOCK, (i + 1) * BLOCK)
        rows = rows_ref[:, i].reshape(halves * rows_half, width)
        acc_t = lax.dot_general(
            w_ref[:, cols], rows, (((0,), (1,)), ((), ())), preferred_element_type=jnp.float32
        )
        acc = acc_t.T + b_ref[:, cols]
        o_ref[i] = jnp.maximum(acc, 0.0).astype(o_ref.dtype)


def encode(rows, weight, bias):
    halves, per_owner, rows_half, width = rows.shape
    group = math.gcd(per_owner, 4)
    return pl.pallas_call(
        encode_kernel,
        grid=(per_owner // group,),
        in_specs=[
            pl.BlockSpec((halves, group, rows_half, width), lambda g: (0, g, 0, 0)),
            pl.BlockSpec((width, group * BLOCK), lambda g: (0, g)),
            pl.BlockSpec((1, group * BLOCK), lambda g: (0, g)),
        ],
        out_specs=pl.BlockSpec((group, halves * rows_half, BLOCK), lambda g: (g, 0, 0)),
        out_shape=jax.ShapeDtypeStruct((per_owner, halves * rows_half, BLOCK), jnp.bfloat16),
    )(rows, weight, bias)


def pair_slots(ids, per_owner, cap):
    layers = ids.shape[0]
    flat = ids.reshape(layers, -1)
    n = flat.shape[1]
    earlier = jnp.arange(n, dtype=jnp.int32)[None, :] < jnp.arange(n, dtype=jnp.int32)[:, None]
    same = (flat[:, :, None] == flat[:, None, :]) & earlier[None]
    rank = jnp.sum(same.astype(jnp.int32), axis=2)
    return (flat * cap + rank).reshape(ids.shape)


def body(residual, targets, block_ids, encoder_weight, encoder_bias, decoder_weight, decoder_bias):
    layer_index = lax.axis_index("layer")
    tok_index = lax.axis_index("tok")
    layers = lax.axis_size("layer")
    tok_count = lax.axis_size("tok")
    tok_rows = residual.shape[1]
    width = residual.shape[2]
    topk = block_ids.shape[2]
    per_owner = encoder_weight.shape[2] // BLOCK
    blocks = per_owner * tok_count
    cap = max(2, 2 * tok_rows * topk // blocks)
    per_src = per_owner * cap
    tokens = tok_rows * tok_count
    slot_count = per_owner * tok_count * cap

    codes_own = pair_slots(block_ids, per_owner, cap)
    codes_all = lax.all_gather(codes_own, "tok", axis=1, tiled=True)
    local = codes_all.reshape(layers, tok_count, tok_rows, topk) - tok_index * per_src
    src_of = jnp.arange(tok_count, dtype=jnp.int32)[:, None]
    slot_of = jnp.where(
        (local >= 0) & (local < per_src),
        (local // cap) * (tok_count * cap) + src_of[None, :, :, None] * cap + local % cap,
        slot_count,
    ).reshape(layers, tokens, topk)
    halves = 2 if (tok_count % 2 == 0 and (tok_count // 2) * cap % 16 == 0) else 1
    rows_half = tok_count * cap // halves
    block_hit = (slot_of // (tok_count * cap))[..., None] == jnp.arange(per_owner, dtype=jnp.int32)
    row_hit = (slot_of % rows_half)[..., None] == jnp.arange(rows_half, dtype=jnp.int32)
    used = slot_of < slot_count
    hits = jnp.any(block_hit[..., :, None] & row_hit[..., None, :] & used[..., None, None], axis=2)

    res_all = lax.all_gather(residual[0], "tok", axis=0, tiled=True)
    own_hits = lax.dynamic_index_in_dim(hits, layer_index, 0, keepdims=False).astype(jnp.bfloat16)
    rows = jnp.einsum(
        "gtbx,gtd->gbxd",
        own_hits.reshape(halves, tokens // halves, per_owner, rows_half),
        res_all.reshape(halves, tokens // halves, width),
        preferred_element_type=jnp.float32,
    ).astype(jnp.bfloat16)
    codes = encode(rows, encoder_weight[0], encoder_bias[0].reshape(1, -1))
    received = [codes] + [
        lax.ppermute(codes, "layer", [(i, i + shift) for i in range(layers - shift)])
        for shift in range(1, layers)
    ]
    shifts = (layer_index - jnp.arange(layers, dtype=jnp.int32)) % layers
    gathered = jnp.take(jnp.stack(received), shifts, axis=0)

    valid = jnp.arange(layers, dtype=jnp.int32) <= layer_index
    combine = (hits & valid[:, None, None, None]).astype(jnp.bfloat16)
    combine = combine.reshape(layers, halves, tokens // halves, per_owner, rows_half)
    weights = decoder_weight[0].reshape(layers, per_owner, BLOCK, width)
    cut = (width // BLOCK) * 2 // 7 * BLOCK if width % BLOCK == 0 else 0
    bounds = [0, cut, width] if 0 < cut < width else [0, width]
    pieces = []
    chunk_codes = gathered
    for lo, hi in zip(bounds[:-1], bounds[1:]):
        terms = jnp.einsum(
            "lbxe,lbed->lbxd",
            chunk_codes,
            weights[..., lo:hi],
            preferred_element_type=jnp.float32,
        ).astype(jnp.bfloat16)
        partial = jnp.einsum(
            "lgtbx,lbgxd->gtd",
            combine,
            terms.reshape(layers, per_owner, halves, rows_half, hi - lo),
            preferred_element_type=jnp.float32,
        ).reshape(tokens, hi - lo).astype(jnp.bfloat16)
        chunk_codes, partial = lax.optimization_barrier((chunk_codes, partial))
        pieces.append(lax.psum_scatter(partial, "tok", scatter_dimension=0, tiled=True))
    summed = jnp.concatenate(pieces, axis=1)
    recon32 = decoder_bias[0][None, :] + summed.astype(jnp.float32)
    difference = recon32 - targets[0].astype(jnp.float32)
    error = jnp.mean(difference * difference, axis=1)
    return (recon32.astype(jnp.bfloat16)[None], error[None])


def solution(mesh):
    in_specs = (
        P("layer", "tok", None),
        P("layer", "tok", None),
        P(None, "tok", None),
        P("layer", None, "tok"),
        P("layer", "tok"),
        P("layer", None, "tok", None),
        P("layer", None),
    )
    out_specs = (P("layer", "tok", None), P("layer", "tok"))
    return jax.shard_map(body, mesh=mesh, in_specs=in_specs, out_specs=out_specs, check_vma=False)
```

```python
import math

import jax
import jax.numpy as jnp
from jax import lax
from jax.experimental import pallas as pl
from jax.sharding import PartitionSpec as P

BLOCK = 128


def encode_kernel(rows_ref, w_ref, b_ref, o_ref):
    halves, group, rows_half, width = rows_ref.shape
    for i in range(group):
        cols = slice(i * BLOCK, (i + 1) * BLOCK)
        rows = rows_ref[:, i].reshape(halves * rows_half, width)
        acc = jnp.dot(rows, w_ref[:, cols], preferred_element_type=jnp.float32)
        acc = acc + b_ref[:, cols]
        o_ref[i] = jnp.maximum(acc, 0.0).astype(o_ref.dtype)


def encode(rows, weight, bias):
    halves, per_owner, rows_half, width = rows.shape
    group = math.gcd(per_owner, 8)
    return pl.pallas_call(
        encode_kernel,
        grid=(per_owner // group,),
        in_specs=[
            pl.BlockSpec((halves, group, rows_half, width), lambda g: (0, g, 0, 0)),
            pl.BlockSpec((width, group * BLOCK), lambda g: (0, g)),
            pl.BlockSpec((1, group * BLOCK), lambda g: (0, g)),
        ],
        out_specs=pl.BlockSpec((group, halves * rows_half, BLOCK), lambda g: (g, 0, 0)),
        out_shape=jax.ShapeDtypeStruct((per_owner, halves * rows_half, BLOCK), jnp.bfloat16),
    )(rows, weight, bias)


def pair_slots(ids, per_owner, cap):
    layers = ids.shape[0]
    flat = ids.reshape(layers, -1)
    n = flat.shape[1]
    earlier = jnp.arange(n, dtype=jnp.int32)[None, :] < jnp.arange(n, dtype=jnp.int32)[:, None]
    same = (flat[:, :, None] == flat[:, None, :]) & earlier[None]
    rank = jnp.sum(same.astype(jnp.int32), axis=2)
    return (flat * cap + rank).reshape(ids.shape)


def body(residual, targets, block_ids, encoder_weight, encoder_bias, decoder_weight, decoder_bias):
    layer_index = lax.axis_index("layer")
    tok_index = lax.axis_index("tok")
    layers = lax.axis_size("layer")
    tok_count = lax.axis_size("tok")
    tok_rows = residual.shape[1]
    width = residual.shape[2]
    topk = block_ids.shape[2]
    per_owner = encoder_weight.shape[2] // BLOCK
    blocks = per_owner * tok_count
    cap = max(2, 2 * tok_rows * topk // blocks)
    per_src = per_owner * cap
    tokens = tok_rows * tok_count
    slot_count = per_owner * tok_count * cap

    codes_own = pair_slots(block_ids, per_owner, cap)
    codes_all = lax.all_gather(codes_own, "tok", axis=1, tiled=True)
    local = codes_all.reshape(layers, tok_count, tok_rows, topk) - tok_index * per_src
    src_of = jnp.arange(tok_count, dtype=jnp.int32)[:, None]
    slot_of = jnp.where(
        (local >= 0) & (local < per_src),
        (local // cap) * (tok_count * cap) + src_of[None, :, :, None] * cap + local % cap,
        slot_count,
    ).reshape(layers, tokens, topk)
    halves = 2 if (tok_count % 2 == 0 and (tok_count // 2) * cap % 16 == 0) else 1
    rows_half = tok_count * cap // halves
    block_hit = (slot_of // (tok_count * cap))[..., None] == jnp.arange(per_owner, dtype=jnp.int32)
    row_hit = (slot_of % rows_half)[..., None] == jnp.arange(rows_half, dtype=jnp.int32)
    used = slot_of < slot_count
    hits = jnp.any(block_hit[..., :, None] & row_hit[..., None, :] & used[..., None, None], axis=2)

    res_all = lax.all_gather(residual[0], "tok", axis=0, tiled=True)
    own_hits = lax.dynamic_index_in_dim(hits, layer_index, 0, keepdims=False).astype(jnp.bfloat16)
    rows = jnp.einsum(
        "gtbx,gtd->gbxd",
        own_hits.reshape(halves, tokens // halves, per_owner, rows_half),
        res_all.reshape(halves, tokens // halves, width),
        preferred_element_type=jnp.float32,
    ).astype(jnp.bfloat16)
    codes = encode(rows, encoder_weight[0], encoder_bias[0].reshape(1, -1))
    received = [codes] + [
        lax.ppermute(codes, "layer", [(i, i + shift) for i in range(layers - shift)])
        for shift in range(1, layers)
    ]
    shifts = (layer_index - jnp.arange(layers, dtype=jnp.int32)) % layers
    gathered = jnp.take(jnp.stack(received), shifts, axis=0)

    valid = jnp.arange(layers, dtype=jnp.int32) <= layer_index
    combine = (hits & valid[:, None, None, None]).astype(jnp.bfloat16)
    combine = combine.reshape(layers, halves, tokens // halves, per_owner, rows_half)
    weights = decoder_weight[0].reshape(layers, per_owner, BLOCK, width)
    cut = (width // BLOCK) * 2 // 7 * BLOCK if width % BLOCK == 0 else 0
    bounds = [0, cut, width] if 0 < cut < width else [0, width]
    pieces = []
    chunk_codes = gathered
    for lo, hi in zip(bounds[:-1], bounds[1:]):
        terms = jnp.einsum(
            "lbxe,lbed->lbxd",
            chunk_codes,
            weights[..., lo:hi],
            preferred_element_type=jnp.float32,
        ).astype(jnp.bfloat16)
        partial = jnp.einsum(
            "lgtbx,lbgxd->gtd",
            combine,
            terms.reshape(layers, per_owner, halves, rows_half, hi - lo),
            preferred_element_type=jnp.float32,
        ).reshape(tokens, hi - lo).astype(jnp.bfloat16)
        chunk_codes, partial = lax.optimization_barrier((chunk_codes, partial))
        pieces.append(lax.psum_scatter(partial, "tok", scatter_dimension=0, tiled=True))
    summed = jnp.concatenate(pieces, axis=1)
    recon32 = decoder_bias[0][None, :] + summed.astype(jnp.float32)
    difference = recon32 - targets[0].astype(jnp.float32)
    error = jnp.mean(difference * difference, axis=1)
    return (recon32.astype(jnp.bfloat16)[None], error[None])


def solution(mesh):
    in_specs = (
        P("layer", "tok", None),
        P("layer", "tok", None),
        P(None, "tok", None),
        P("layer", None, "tok"),
        P("layer", "tok"),
        P("layer", None, "tok", None),
        P("layer", None),
    )
    out_specs = (P("layer", "tok", None), P("layer", "tok"))
    return jax.shard_map(body, mesh=mesh, in_specs=in_specs, out_specs=out_specs, check_vma=False)
```

```python
import math

import jax
import jax.numpy as jnp
from jax import lax
from jax.experimental import pallas as pl
from jax.sharding import PartitionSpec as P

BLOCK = 128


def encode_kernel(rows_ref, w_ref, b_ref, o_ref):
    halves, group, rows_half, width = rows_ref.shape
    for i in range(group):
        cols = slice(i * BLOCK, (i + 1) * BLOCK)
        rows = rows_ref[:, i].reshape(halves * rows_half, width)
        acc = jnp.dot(rows, w_ref[:, cols], preferred_element_type=jnp.float32)
        acc = acc + b_ref[:, cols]
        o_ref[i] = jnp.maximum(acc, 0.0).astype(o_ref.dtype)


def encode(rows, weight, bias):
    halves, per_owner, rows_half, width = rows.shape
    group = math.gcd(per_owner, 4)
    return pl.pallas_call(
        encode_kernel,
        grid=(per_owner // group,),
        in_specs=[
            pl.BlockSpec((halves, group, rows_half, width), lambda g: (0, g, 0, 0)),
            pl.BlockSpec((width, group * BLOCK), lambda g: (0, g)),
            pl.BlockSpec((1, group * BLOCK), lambda g: (0, g)),
        ],
        out_specs=pl.BlockSpec((group, halves * rows_half, BLOCK), lambda g: (g, 0, 0)),
        out_shape=jax.ShapeDtypeStruct((per_owner, halves * rows_half, BLOCK), jnp.bfloat16),
    )(rows, weight, bias)


def pair_slots(ids, per_owner, cap):
    layers = ids.shape[0]
    flat = ids.reshape(layers, -1)
    n = flat.shape[1]
    earlier = jnp.arange(n, dtype=jnp.int32)[None, :] < jnp.arange(n, dtype=jnp.int32)[:, None]
    same = (flat[:, :, None] == flat[:, None, :]) & earlier[None]
    rank = jnp.sum(same.astype(jnp.int32), axis=2)
    return (flat * cap + rank).reshape(ids.shape)


def body(residual, targets, block_ids, encoder_weight, encoder_bias, decoder_weight, decoder_bias):
    layer_index = lax.axis_index("layer")
    tok_index = lax.axis_index("tok")
    layers = lax.axis_size("layer")
    tok_count = lax.axis_size("tok")
    tok_rows = residual.shape[1]
    width = residual.shape[2]
    topk = block_ids.shape[2]
    per_owner = encoder_weight.shape[2] // BLOCK
    blocks = per_owner * tok_count
    cap = max(2, 2 * tok_rows * topk // blocks)
    per_src = per_owner * cap
    tokens = tok_rows * tok_count
    slot_count = per_owner * tok_count * cap

    codes_own = pair_slots(block_ids, per_owner, cap)
    codes_all = lax.all_gather(codes_own, "tok", axis=1, tiled=True)
    local = codes_all.reshape(layers, tok_count, tok_rows, topk) - tok_index * per_src
    src_of = jnp.arange(tok_count, dtype=jnp.int32)[:, None]
    slot_of = jnp.where(
        (local >= 0) & (local < per_src),
        (local // cap) * (tok_count * cap) + src_of[None, :, :, None] * cap + local % cap,
        slot_count,
    ).reshape(layers, tokens, topk)
    halves = 2 if (tok_count % 2 == 0 and (tok_count // 2) * cap % 16 == 0) else 1
    rows_half = tok_count * cap // halves
    block_hit = (slot_of // (tok_count * cap))[..., None] == jnp.arange(per_owner, dtype=jnp.int32)
    row_hit = (slot_of % rows_half)[..., None] == jnp.arange(rows_half, dtype=jnp.int32)
    used = slot_of < slot_count
    hits = jnp.any(block_hit[..., :, None] & row_hit[..., None, :] & used[..., None, None], axis=2)

    res_all = lax.all_gather(residual[0], "tok", axis=0, tiled=True)
    own_hits = lax.dynamic_index_in_dim(hits, layer_index, 0, keepdims=False).astype(jnp.bfloat16)
    own_hits = own_hits.reshape(halves, tokens // halves, per_owner, rows_half).transpose(0, 2, 3, 1)
    own_hits = lax.optimization_barrier(own_hits)
    rows = jnp.einsum(
        "gbxt,gtd->gbxd",
        own_hits,
        res_all.reshape(halves, tokens // halves, width),
        preferred_element_type=jnp.float32,
    ).astype(jnp.bfloat16)
    codes = encode(rows, encoder_weight[0], encoder_bias[0].reshape(1, -1))
    received = [codes] + [
        lax.ppermute(codes, "layer", [(i, i + shift) for i in range(layers - shift)])
        for shift in range(1, layers)
    ]
    shifts = (layer_index - jnp.arange(layers, dtype=jnp.int32)) % layers
    gathered = jnp.take(jnp.stack(received), shifts, axis=0)

    valid = jnp.arange(layers, dtype=jnp.int32) <= layer_index
    combine = (hits & valid[:, None, None, None]).astype(jnp.bfloat16)
    combine = combine.reshape(layers, halves, tokens // halves, per_owner, rows_half)
    weights = decoder_weight[0].reshape(layers, per_owner, BLOCK, width)
    cut = (width // BLOCK) * 2 // 7 * BLOCK if width % BLOCK == 0 else 0
    bounds = [0, cut, width] if 0 < cut < width else [0, width]
    pieces = []
    chunk_codes = gathered
    for lo, hi in zip(bounds[:-1], bounds[1:]):
        terms = jnp.einsum(
            "lbxe,lbed->lbxd",
            chunk_codes,
            weights[..., lo:hi],
            preferred_element_type=jnp.float32,
        ).astype(jnp.bfloat16)
        partial = jnp.einsum(
            "lgtbx,lbgxd->gtd",
            combine,
            terms.reshape(layers, per_owner, halves, rows_half, hi - lo),
            preferred_element_type=jnp.float32,
        ).reshape(tokens, hi - lo).astype(jnp.bfloat16)
        chunk_codes, partial = lax.optimization_barrier((chunk_codes, partial))
        pieces.append(lax.psum_scatter(partial, "tok", scatter_dimension=0, tiled=True))
    summed = jnp.concatenate(pieces, axis=1)
    recon32 = decoder_bias[0][None, :] + summed.astype(jnp.float32)
    difference = recon32 - targets[0].astype(jnp.float32)
    error = jnp.mean(difference * difference, axis=1)
    return (recon32.astype(jnp.bfloat16)[None], error[None])


def solution(mesh):
    in_specs = (
        P("layer", "tok", None),
        P("layer", "tok", None),
        P(None, "tok", None),
        P("layer", None, "tok"),
        P("layer", "tok"),
        P("layer", None, "tok", None),
        P("layer", None),
    )
    out_specs = (P("layer", "tok", None), P("layer", "tok"))
    return jax.shard_map(body, mesh=mesh, in_specs=in_specs, out_specs=out_specs, check_vma=False)
```

```python
import math

import jax
import jax.numpy as jnp
from jax import lax
from jax.experimental import pallas as pl
from jax.sharding import PartitionSpec as P

BLOCK = 128


def encode_kernel(rows_ref, w_ref, b_ref, o_ref):
    halves, group, rows_half, width = rows_ref.shape
    for i in range(group):
        cols = slice(i * BLOCK, (i + 1) * BLOCK)
        rows = rows_ref[:, i].reshape(halves * rows_half, width)
        acc = jnp.dot(rows, w_ref[:, cols], preferred_element_type=jnp.float32)
        acc = acc + b_ref[:, cols]
        o_ref[i] = jnp.maximum(acc, 0.0).astype(o_ref.dtype)


def encode(rows, weight, bias):
    halves, per_owner, rows_half, width = rows.shape
    group = math.gcd(per_owner, 4)
    return pl.pallas_call(
        encode_kernel,
        grid=(per_owner // group,),
        in_specs=[
            pl.BlockSpec((halves, group, rows_half, width), lambda g: (0, g, 0, 0)),
            pl.BlockSpec((width, group * BLOCK), lambda g: (0, g)),
            pl.BlockSpec((1, group * BLOCK), lambda g: (0, g)),
        ],
        out_specs=pl.BlockSpec((group, halves * rows_half, BLOCK), lambda g: (g, 0, 0)),
        out_shape=jax.ShapeDtypeStruct((per_owner, halves * rows_half, BLOCK), jnp.bfloat16),
    )(rows, weight, bias)


def pair_slots(ids, per_owner, cap):
    layers = ids.shape[0]
    flat = ids.reshape(layers, -1)
    n = flat.shape[1]
    earlier = jnp.arange(n, dtype=jnp.int32)[None, :] < jnp.arange(n, dtype=jnp.int32)[:, None]
    same = (flat[:, :, None] == flat[:, None, :]) & earlier[None]
    rank = jnp.sum(same.astype(jnp.int32), axis=2)
    return (flat * cap + rank).reshape(ids.shape)


def body(residual, targets, block_ids, encoder_weight, encoder_bias, decoder_weight, decoder_bias):
    layer_index = lax.axis_index("layer")
    tok_index = lax.axis_index("tok")
    layers = lax.axis_size("layer")
    tok_count = lax.axis_size("tok")
    tok_rows = residual.shape[1]
    width = residual.shape[2]
    topk = block_ids.shape[2]
    per_owner = encoder_weight.shape[2] // BLOCK
    blocks = per_owner * tok_count
    cap = max(2, 2 * tok_rows * topk // blocks)
    per_src = per_owner * cap
    tokens = tok_rows * tok_count
    slot_count = per_owner * tok_count * cap

    codes_own = pair_slots(block_ids, per_owner, cap)
    codes_all = lax.all_gather(codes_own, "tok", axis=1, tiled=True)
    local = codes_all.reshape(layers, tok_count, tok_rows, topk) - tok_index * per_src
    src_of = jnp.arange(tok_count, dtype=jnp.int32)[:, None]
    slot_of = jnp.where(
        (local >= 0) & (local < per_src),
        (local // cap) * (tok_count * cap) + src_of[None, :, :, None] * cap + local % cap,
        slot_count,
    ).reshape(layers, tokens, topk)
    halves = 2 if (tok_count % 2 == 0 and (tok_count // 2) * cap % 16 == 0) else 1
    rows_half = tok_count * cap // halves
    block_hit = (slot_of // (tok_count * cap))[..., None] == jnp.arange(per_owner, dtype=jnp.int32)
    row_hit = (slot_of % rows_half)[..., None] == jnp.arange(rows_half, dtype=jnp.int32)
    used = slot_of < slot_count
    hits = jnp.any(block_hit[..., :, None] & row_hit[..., None, :] & used[..., None, None], axis=2)

    res_all = lax.all_gather(residual[0], "tok", axis=0, tiled=True)
    own_hits = lax.dynamic_index_in_dim(hits, layer_index, 0, keepdims=False).astype(jnp.bfloat16)
    own_hits = own_hits.reshape(halves, tokens // halves, per_owner, rows_half).transpose(0, 2, 3, 1)
    own_hits = lax.optimization_barrier(own_hits)
    rows = jnp.einsum(
        "gbxt,gtd->gbxd",
        own_hits,
        res_all.reshape(halves, tokens // halves, width),
        preferred_element_type=jnp.float32,
    ).astype(jnp.bfloat16)
    codes = encode(rows, encoder_weight[0], encoder_bias[0].reshape(1, -1))
    received = [codes] + [
        lax.ppermute(codes, "layer", [(i, i + shift) for i in range(layers - shift)])
        for shift in range(1, layers)
    ]
    shifts = (layer_index - jnp.arange(layers, dtype=jnp.int32)) % layers
    gathered = jnp.take(jnp.stack(received), shifts, axis=0)

    valid = jnp.arange(layers, dtype=jnp.int32) <= layer_index
    combine = (hits & valid[:, None, None, None]).astype(jnp.bfloat16)
    combine = combine.reshape(layers, halves, tokens // halves, per_owner, rows_half)
    weights = decoder_weight[0].reshape(layers, per_owner, BLOCK, width)
    cut = (width // BLOCK) // 4 * BLOCK if width % BLOCK == 0 else 0
    bounds = [0, cut, width] if 0 < cut < width else [0, width]
    pieces = []
    chunk_codes = gathered
    for lo, hi in zip(bounds[:-1], bounds[1:]):
        terms = jnp.einsum(
            "lbxe,lbed->lbxd",
            chunk_codes,
            weights[..., lo:hi],
            preferred_element_type=jnp.float32,
        ).astype(jnp.bfloat16)
        partial = jnp.einsum(
            "lgtbx,lbgxd->gtd",
            combine,
            terms.reshape(layers, per_owner, halves, rows_half, hi - lo),
            preferred_element_type=jnp.float32,
        ).reshape(tokens, hi - lo).astype(jnp.bfloat16)
        chunk_codes, partial = lax.optimization_barrier((chunk_codes, partial))
        pieces.append(lax.psum_scatter(partial, "tok", scatter_dimension=0, tiled=True))
    summed = jnp.concatenate(pieces, axis=1)
    recon32 = decoder_bias[0][None, :] + summed.astype(jnp.float32)
    difference = recon32 - targets[0].astype(jnp.float32)
    error = jnp.mean(difference * difference, axis=1)
    return (recon32.astype(jnp.bfloat16)[None], error[None])


def solution(mesh):
    in_specs = (
        P("layer", "tok", None),
        P("layer", "tok", None),
        P(None, "tok", None),
        P("layer", None, "tok"),
        P("layer", "tok"),
        P("layer", None, "tok", None),
        P("layer", None),
    )
    out_specs = (P("layer", "tok", None), P("layer", "tok"))
    return jax.shard_map(body, mesh=mesh, in_specs=in_specs, out_specs=out_specs, check_vma=False)
```

```python
import math

import jax
import jax.numpy as jnp
from jax import lax
from jax.experimental import pallas as pl
from jax.sharding import PartitionSpec as P

BLOCK = 128


def encode_kernel(rows_ref, w_ref, b_ref, o_ref):
    halves, group, rows_half, width = rows_ref.shape
    for i in range(group):
        cols = slice(i * BLOCK, (i + 1) * BLOCK)
        rows = rows_ref[:, i].reshape(halves * rows_half, width)
        acc = jnp.dot(rows, w_ref[:, cols], preferred_element_type=jnp.float32)
        acc = acc + b_ref[:, cols]
        o_ref[i] = jnp.maximum(acc, 0.0).astype(o_ref.dtype)


def encode(rows, weight, bias):
    halves, per_owner, rows_half, width = rows.shape
    group = math.gcd(per_owner, 4)
    return pl.pallas_call(
        encode_kernel,
        grid=(per_owner // group,),
        in_specs=[
            pl.BlockSpec((halves, group, rows_half, width), lambda g: (0, g, 0, 0)),
            pl.BlockSpec((width, group * BLOCK), lambda g: (0, g)),
            pl.BlockSpec((1, group * BLOCK), lambda g: (0, g)),
        ],
        out_specs=pl.BlockSpec((group, halves * rows_half, BLOCK), lambda g: (g, 0, 0)),
        out_shape=jax.ShapeDtypeStruct((per_owner, halves * rows_half, BLOCK), jnp.bfloat16),
    )(rows, weight, bias)


def pair_slots(ids, per_owner, cap):
    layers = ids.shape[0]
    flat = ids.reshape(layers, -1)
    n = flat.shape[1]
    earlier = jnp.arange(n, dtype=jnp.int32)[None, :] < jnp.arange(n, dtype=jnp.int32)[:, None]
    same = (flat[:, :, None] == flat[:, None, :]) & earlier[None]
    rank = jnp.sum(same.astype(jnp.int32), axis=2)
    return (flat * cap + rank).reshape(ids.shape)


def body(residual, targets, block_ids, encoder_weight, encoder_bias, decoder_weight, decoder_bias):
    layer_index = lax.axis_index("layer")
    tok_index = lax.axis_index("tok")
    layers = lax.axis_size("layer")
    tok_count = lax.axis_size("tok")
    tok_rows = residual.shape[1]
    width = residual.shape[2]
    topk = block_ids.shape[2]
    per_owner = encoder_weight.shape[2] // BLOCK
    blocks = per_owner * tok_count
    cap = max(2, 2 * tok_rows * topk // blocks)
    per_src = per_owner * cap
    tokens = tok_rows * tok_count
    slot_count = per_owner * tok_count * cap

    codes_own = pair_slots(block_ids, per_owner, cap)
    codes_all = lax.all_gather(codes_own, "tok", axis=1, tiled=True)
    local = codes_all.reshape(layers, tok_count, tok_rows, topk) - tok_index * per_src
    src_of = jnp.arange(tok_count, dtype=jnp.int32)[:, None]
    slot_of = jnp.where(
        (local >= 0) & (local < per_src),
        (local // cap) * (tok_count * cap) + src_of[None, :, :, None] * cap + local % cap,
        slot_count,
    ).reshape(layers, tokens, topk)
    halves = 2 if (tok_count % 2 == 0 and (tok_count // 2) * cap % 16 == 0) else 1
    rows_half = tok_count * cap // halves
    block_hit = (slot_of // (tok_count * cap))[..., None] == jnp.arange(per_owner, dtype=jnp.int32)
    row_hit = (slot_of % rows_half)[..., None] == jnp.arange(rows_half, dtype=jnp.int32)
    used = slot_of < slot_count
    hits = jnp.any(block_hit[..., :, None] & row_hit[..., None, :] & used[..., None, None], axis=2)

    res_all = lax.all_gather(residual[0], "tok", axis=0, tiled=True)
    own_hits = lax.dynamic_index_in_dim(hits, layer_index, 0, keepdims=False).astype(jnp.bfloat16)
    own_hits = own_hits.reshape(halves, tokens // halves, per_owner, rows_half).transpose(0, 2, 3, 1)
    own_hits = lax.optimization_barrier(own_hits)
    rows = jnp.einsum(
        "gbxt,gtd->gbxd",
        own_hits,
        res_all.reshape(halves, tokens // halves, width),
        preferred_element_type=jnp.float32,
    ).astype(jnp.bfloat16)
    codes = encode(rows, encoder_weight[0], encoder_bias[0].reshape(1, -1))
    gathered = lax.all_gather(codes, "layer", axis=0, tiled=False)

    valid = jnp.arange(layers, dtype=jnp.int32) <= layer_index
    combine = (hits & valid[:, None, None, None]).astype(jnp.bfloat16)
    combine = combine.reshape(layers, halves, tokens // halves, per_owner, rows_half)
    weights = decoder_weight[0].reshape(layers, per_owner, BLOCK, width)
    cut = (width // BLOCK) * 2 // 7 * BLOCK if width % BLOCK == 0 else 0
    bounds = [0, cut, width] if 0 < cut < width else [0, width]
    pieces = []
    chunk_codes = gathered
    for lo, hi in zip(bounds[:-1], bounds[1:]):
        terms = jnp.einsum(
            "lbxe,lbed->lbxd",
            chunk_codes,
            weights[..., lo:hi],
            preferred_element_type=jnp.float32,
        ).astype(jnp.bfloat16)
        partial = jnp.einsum(
            "lgtbx,lbgxd->gtd",
            combine,
            terms.reshape(layers, per_owner, halves, rows_half, hi - lo),
            preferred_element_type=jnp.float32,
        ).reshape(tokens, hi - lo).astype(jnp.bfloat16)
        chunk_codes, partial = lax.optimization_barrier((chunk_codes, partial))
        pieces.append(lax.psum_scatter(partial, "tok", scatter_dimension=0, tiled=True))
    summed = jnp.concatenate(pieces, axis=1)
    recon32 = decoder_bias[0][None, :] + summed.astype(jnp.float32)
    difference = recon32 - targets[0].astype(jnp.float32)
    error = jnp.mean(difference * difference, axis=1)
    return (recon32.astype(jnp.bfloat16)[None], error[None])


def solution(mesh):
    in_specs = (
        P("layer", "tok", None),
        P("layer", "tok", None),
        P(None, "tok", None),
        P("layer", None, "tok"),
        P("layer", "tok"),
        P("layer", None, "tok", None),
        P("layer", None),
    )
    out_specs = (P("layer", "tok", None), P("layer", "tok"))
    return jax.shard_map(body, mesh=mesh, in_specs=in_specs, out_specs=out_specs, check_vma=False)
```
